32 devices in a mesh: dp: 16 (over z, y, x), lat: 2 (over core).
Axes of the slice: x: 2, y: 2, z: 4, core: 2. Of those that a mesh axis runs over, the one named last changes fastest.
Arguments:
- acts: bfloat16 [2048, 8192], P('dp', 'lat'), may hold values from -6 to 6
- owner_ids: int32 [2048, 4], P('dp'), may hold values from 0 to 31, all different within a row; in each aligned block of 128 rows (0 to 127, 128 to 255, ...) at most 32 rows name the same one
- block_codes: int32 [2048, 4], P('dp'), may hold values from 1 to 3
- weights: bfloat16 [4096, 8192], P(('dp', 'lat')), may hold values from -0.25 to 0.25
- enc_bias: float32 [4096], P(('dp', 'lat')), may hold values from -3 to 3
- dec_bias: float32 [8192], P('lat'), may hold values from -3 to 3
Outputs:
- recon: bfloat16 [2048, 8192], P('dp', 'lat')
- grad_weights: bfloat16 [4096, 8192], P(('dp', 'lat'))
- grad_enc_bias: float32 [4096], P(('dp', 'lat'))
- grad_dec_bias: float32 [8192], P('lat')
The draws below stay inside these ranges and needn't reach their ends.
Inputs may be any that keep to these rules, and one draw needn't show every extreme that they name: `owner_ids`: each row names 4 different devices; in each aligned block of 128 rows (the rows of one index of dp) no device is named by more than 32 rows, and some device is named by exactly 32. `block_codes`: bit j (j < 2) of an entry says whether block j of that device's 2 blocks is active for the token.
All inputs are finite; a program needn't handle non-finite values.
Results may differ from the reference program's by a relative error of at most 0.0056.
Values may be sent and summed in bfloat16 or wider, within the bound.
No kernel may reach another device: no remote copies, remote signals or barrier semaphores. Data moves between devices by JAX's collectives and lax.ppermute only.
A program may use at most 192 MiB of HBM per device.

```python
import math
import jax
import jax.numpy as jnp
import numpy as np
from jax import lax

D = 8192
BLOCK = 64
BLK_DEV = 2
KO = 4
TOK_DEV = 128
CAPD = 32
TOKENS = 2048
LAT = 4096
N_DP = 16
N_LAT = 2
DEVICES = 32


def with_ends(values, stream_key, low, largest):
    longest = values.shape.index(max(values.shape))
    spots = []
    for shift in (0, 1):
        where = [jax.random.randint(jax.random.fold_in(stream_key, axis), (), 0, length) for axis, length in enumerate(values.shape)]
        where[longest] = (where[longest] + shift) % values.shape[longest]
        spots.append(tuple(where))
    return values.at[spots[0]].set(low).at[spots[1]].set(largest)


def block_levels(key, dims, shards, low, high):
    loudness, own = 1.0, jax.random.fold_in(key, 6)
    for position, blocks in shards:
        draws = jnp.exp(jax.random.uniform(jax.random.fold_in(own, position), (blocks,), jnp.float32, low / len(shards), high / len(shards)))
        loudness = loudness * jnp.repeat(draws, dims[position] // blocks).reshape([-1 if axis == position else 1 for axis in range(len(dims))])
    return loudness


def routed_block(stream_key, own, number, rows, number_of, top, reach, skew):
    order = jax.random.permutation(stream_key, number_of)
    crowded, usual = shares(number_of, rows * top, reach, skew, True), shares(number_of, rows * top, reach, skew, False)
    places = jnp.arange(number_of)

    def named(lengths, rotation):
        used = int((lengths > 0).sum())
        fixed = max(1, used // 4)
        passed = fixed + (places - fixed + rotation * (used - fixed)) % max(1, number_of - fixed)
        return jnp.zeros((number_of,), jnp.int32).at[order[jnp.where(places < fixed, places, passed)]].set(jnp.asarray(lengths, jnp.int32))

    lengths = jnp.where(number % 4 == 0, named(crowded, number // 4), named(usual, number - number // 4 - 1))
    mixed = jax.random.permutation(jax.random.fold_in(own, 3), number_of)
    source_of, taker = mixed[0:number_of // 2 * 2:2], mixed[1:number_of // 2 * 2:2]
    slack = jnp.minimum(lengths[source_of] - 1, reach - lengths[taker]) // 2
    slack = jnp.where((source_of == order[0]) | (taker == order[0]) | (lengths[taker] == 0), 0, jnp.maximum(slack, 0))
    passed = jax.random.randint(jax.random.fold_in(own, 4), (number_of // 2,), 0, 1 << 20) % (slack + 1)
    lengths = lengths.at[source_of].add(-passed).at[taker].add(passed)
    items = jnp.searchsorted(jnp.cumsum(lengths), jnp.arange(rows * top), side="right").astype(jnp.int32)
    table = items.reshape(top, rows).T
    table = table[jax.random.permutation(jax.random.fold_in(own, 1), rows)]
    rotation = jax.random.randint(jax.random.fold_in(own, 2), (rows, 1), 0, top)
    return jnp.take_along_axis(table, (jnp.arange(top)[None, :] + rotation) % top, axis=1)


def shares(count, total, most, slope, full):
    portions = [(1 << 20) // math.isqrt(grade ** slope) + 1 for grade in range(1, count + 1)]
    largest = most if full else min(most, max(-(-total // count), total * portions[0] // sum(portions)))
    least = 1 if total - largest >= count - 1 else 0
    given, surplus = [largest] + [least] * (count - 1), total - largest - least * (count - 1)
    while surplus > 0:
        free = [i for i in range(1, count) if given[i] < largest] or [i for i in range(1, count) if given[i] < most]
        pool, remaining = sum([portions[i] for i in free]), surplus
        for i in free:
            extra = min(most - given[i], max(1, remaining * portions[i] // pool), surplus)
            given[i] = given[i] + extra
            surplus = surplus - extra
    return np.array(given)


def centred(rng, shape, deviation, reach, cuts=(), kind=jnp.bfloat16):
    loudness = block_levels(rng, shape, cuts, -0.22, 0.18) if cuts else 1.0
    result = jax.random.normal(rng, shape, jnp.float32) * deviation * loudness
    return jnp.minimum(jnp.maximum(result, -reach), reach).astype(kind)


def setup_inputs(seed: int = 0) -> dict:
    streams_of = jax.random.split(jax.random.key(seed), 7)
    acts = centred(streams_of[0], (TOKENS, D), 1.0, 6.0, ((0, 16), (1, 2)))
    owner_ids_keys = jax.random.split(jax.random.fold_in(streams_of[1], 1), TOKENS // TOK_DEV)
    owner_ids_turns = jax.random.permutation(jax.random.fold_in(streams_of[1], 3), TOKENS // TOK_DEV)
    owner_ids = jax.vmap(lambda own, number: routed_block(jax.random.fold_in(streams_of[1], 2), own, number, TOK_DEV, DEVICES, KO, CAPD, 2))(owner_ids_keys, owner_ids_turns).reshape((TOKENS, KO))
    block_codes = with_ends(jax.random.randint(streams_of[2], (TOKENS, KO), 1, 2 ** BLK_DEV), jax.random.fold_in(streams_of[2], 1), 1, (2 ** BLK_DEV) - 1).astype(jnp.int32)
    weights = centred(streams_of[3], (LAT, D), (D // 16) ** -0.5, 0.25, ((0, 32),))
    enc_bias = centred(streams_of[4], (LAT,), 0.5, 3.0, ((0, 32),), jnp.float32)
    dec_bias = centred(streams_of[5], (D,), 0.5, 3.0, ((0, 2),), jnp.float32)
    return dict(acts=acts, owner_ids=owner_ids, block_codes=block_codes, weights=weights, enc_bias=enc_bias, dec_bias=dec_bias)


def owner_work(rows, gate, weight_rows, bias_rows):
    pre = lax.dot_general(rows, weight_rows, (((1,), (1,)), ((), ())), preferred_element_type=jnp.float32) + bias_rows[None, :]
    gate_lat = jnp.repeat(gate, BLOCK, axis=1)
    codes = (jnp.maximum(pre, 0.0) * gate_lat).astype(jnp.bfloat16)
    parts = jnp.dot(codes, weight_rows, preferred_element_type=jnp.float32).astype(jnp.bfloat16)
    return pre, gate_lat, codes, parts


def owner_grads(rows, errors, weight_rows, pre, gate_lat, codes):
    gcodes = lax.dot_general(errors, weight_rows, (((1,), (1,)), ((), ())), preferred_element_type=jnp.float32)
    gpre = gcodes * gate_lat * (pre > 0.0).astype(jnp.float32)
    grad_w = lax.dot_general(codes, errors, (((0,), (0,)), ((), ())), preferred_element_type=jnp.float32)
    grad_w = grad_w + lax.dot_general(gpre.astype(jnp.bfloat16), rows, (((0,), (0,)), ((), ())), preferred_element_type=jnp.float32)
    return grad_w.astype(jnp.bfloat16), jnp.sum(gpre, axis=0)


def code_gates(codes_int):
    return jnp.stack([((codes_int // (2 ** j)) % 2) for j in range(BLK_DEV)], axis=-1).astype(jnp.float32)


def reference(acts, owner_ids, block_codes, weights, enc_bias, dec_bias):
    owner_total = N_DP * N_LAT
    lat_own = BLK_DEV * BLOCK
    ids = owner_ids.reshape(N_DP, TOK_DEV, KO)
    onehot = (ids[..., None] == jnp.arange(owner_total, dtype=jnp.int32)).astype(jnp.int32)
    present = jnp.sum(onehot, axis=2)
    before = jnp.cumsum(present, axis=1) - present
    slot_of = jnp.sum(onehot * before[:, :, None, :], axis=3).astype(jnp.int32)
    group = jnp.arange(N_DP, dtype=jnp.int32)[:, None, None]
    token = group * TOK_DEV + jnp.arange(TOK_DEV, dtype=jnp.int32)[None, :, None] + jnp.zeros_like(ids)
    target = ((ids * N_DP + group) * CAPD + slot_of).reshape(-1).astype(jnp.int32)
    table_size = owner_total * N_DP * CAPD
    token_at = jnp.zeros((table_size,), jnp.int32).at[target].set(token.reshape(-1).astype(jnp.int32))
    token_at = token_at.reshape(owner_total, N_DP * CAPD)
    code_at = jnp.zeros((table_size,), jnp.int32).at[target].set(block_codes.reshape(-1).astype(jnp.int32))
    code_at = code_at.reshape(owner_total, N_DP * CAPD)

    def forward(total, owner):
        index_rows = token_at[owner]
        rows = jnp.take(acts, index_rows, axis=0)
        weight_rows = lax.dynamic_slice_in_dim(weights, (owner * lat_own).astype(jnp.int32), lat_own, 0)
        bias_rows = lax.dynamic_slice_in_dim(enc_bias, (owner * lat_own).astype(jnp.int32), lat_own, 0)
        pre, gate_lat, codes, parts = owner_work(rows, code_gates(code_at[owner]), weight_rows, bias_rows)
        total = total.at[index_rows].add(parts.astype(jnp.float32))
        return total, (pre, codes)

    owners_list = jnp.arange(owner_total, dtype=jnp.int32)
    start = jnp.zeros((TOKENS, D), jnp.float32)
    summed, saved = lax.scan(forward, start, owners_list)
    full = summed + dec_bias[None, :]
    recon = full.astype(jnp.bfloat16)
    err = full - acts.astype(jnp.float32)
    gerr = err.astype(jnp.bfloat16)

    def backward(items):
        owner, pre, codes = items
        index_rows = token_at[owner]
        rows = jnp.take(acts, index_rows, axis=0)
        errors = jnp.take(gerr, index_rows, axis=0)
        weight_rows = lax.dynamic_slice_in_dim(weights, (owner * lat_own).astype(jnp.int32), lat_own, 0)
        gate_lat = jnp.repeat(code_gates(code_at[owner]), BLOCK, axis=1)
        return owner_grads(rows, errors, weight_rows, pre, gate_lat, codes)

    grad_w, grad_b = lax.map(backward, (owners_list, saved[0], saved[1]))
    grad_weights = grad_w.reshape(owner_total * lat_own, D)
    grad_enc_bias = grad_b.reshape(owner_total * lat_own)
    grad_dec_bias = jnp.sum(err, axis=0)
    return recon, grad_weights, grad_enc_bias, grad_dec_bias
```

```python
import jax
import jax.numpy as jnp
from jax import lax
from jax.sharding import PartitionSpec as P

BLK_DEV = 2
ALL = ("dp", "lat")


def slot_tables(ids, owner_total, block_rows, slot_cap):
    tokens, own_count = ids.shape
    blocks = tokens // block_rows
    per_owner = blocks * slot_cap
    onehot = (ids[:, :, None] == jnp.arange(owner_total, dtype=jnp.int32)[None, None, :]).astype(
        jnp.int32
    )
    present = jnp.sum(onehot, axis=1).reshape(blocks, block_rows, owner_total)
    before = (jnp.cumsum(present, axis=1) - present).reshape(tokens, owner_total)
    rank = jnp.take_along_axis(before, ids, axis=1)
    block = (jnp.arange(tokens, dtype=jnp.int32) // block_rows)[:, None]
    slot = ids * per_owner + block * slot_cap + rank
    slot_flat = slot.reshape(-1)
    pair_index = jnp.arange(tokens * own_count, dtype=jnp.int32)
    total = owner_total * per_owner
    pair_at = jnp.zeros((total,), jnp.int32).at[slot_flat].set(pair_index, unique_indices=True)
    valid = jnp.zeros((total,), jnp.bool_).at[slot_flat].set(True, unique_indices=True)
    return slot_flat, pair_at, valid, per_owner


def local(acts, owner_ids, block_codes, weights, enc_bias, dec_bias):
    dp_count = lax.axis_size("dp")
    lat_count = lax.axis_size("lat")
    dp_idx = lax.axis_index("dp")
    lat_idx = lax.axis_index("lat")
    owner_total = dp_count * lat_count
    tok_rows, own_count = owner_ids.shape
    half = acts.shape[1]
    full_width = weights.shape[1]
    lat_own = weights.shape[0]
    block_width = lat_own // BLK_DEV
    fs = half // dp_count
    mine_rows = tok_rows // lat_count
    tokens = tok_rows * dp_count
    slot_cap = max(2, 2 * tok_rows * own_count // owner_total)

    acts_fs = lax.all_to_all(
        acts.reshape(tok_rows, dp_count, fs).transpose(1, 0, 2), "dp", 0, 0, tiled=True
    ).reshape(tokens, fs)
    w_send = (
        weights.reshape(lat_own, lat_count, dp_count, fs)
        .transpose(2, 1, 0, 3)
        .reshape(owner_total, lat_own, fs)
    )
    w_fs = lax.all_to_all(w_send, ALL, 0, 0, tiled=True)

    ids_all = lax.all_gather(owner_ids, "dp", axis=0, tiled=True)
    slot_flat, pair_at, valid, per_owner = slot_tables(ids_all, owner_total, tok_rows, slot_cap)
    tok_at = pair_at // own_count
    valid_col = valid[:, None]

    def to_slots(x_fs):
        return jnp.where(valid_col, jnp.take(x_fs, tok_at, axis=0, mode="clip"), 0).reshape(
            owner_total, per_owner, fs
        )

    def slots_to_pairs(v):
        return jnp.take(v.reshape(owner_total * per_owner, -1), slot_flat, axis=0, mode="clip").reshape(
            tokens, own_count, -1
        )

    def pairs_to_slots(x):
        flat = x.reshape(tokens * own_count, -1)
        return jnp.where(valid_col, jnp.take(flat, pair_at, axis=0, mode="clip"), 0).reshape(
            owner_total, per_owner, -1
        )

    acts_slots = to_slots(acts_fs)
    pre_part = jnp.einsum("ocf,olf->ocl", acts_slots, w_fs, preferred_element_type=jnp.float32)
    pre_sum = lax.psum_scatter(slots_to_pairs(pre_part), ALL, scatter_dimension=0, tiled=True)

    start = lat_idx * mine_rows
    my_ids = lax.dynamic_slice_in_dim(owner_ids, start, mine_rows, 0)
    my_codes = lax.dynamic_slice_in_dim(block_codes, start, mine_rows, 0)
    enc_all = lax.all_gather(enc_bias, ALL, axis=0, tiled=True).reshape(owner_total, lat_own)
    pre = pre_sum + jnp.take(enc_all, my_ids, axis=0, mode="clip")
    lat_block = jnp.arange(lat_own, dtype=jnp.int32) // block_width
    gate = ((my_codes[:, :, None] // (2 ** lat_block)[None, None, :]) % 2).astype(jnp.float32)
    codes = (jnp.maximum(pre, 0.0) * gate).astype(jnp.bfloat16)

    codes_all = lax.all_gather(codes, ALL, axis=0, tiled=True)
    codes_slots = pairs_to_slots(codes_all)
    contrib = jnp.einsum("ocl,olf->ocf", codes_slots, w_fs, preferred_element_type=jnp.float32)
    summed = jnp.sum(slots_to_pairs(contrib), axis=1)
    bias_fs = lax.dynamic_slice_in_dim(dec_bias, dp_idx * fs, fs, 0)
    full = summed + bias_fs[None, :]
    err = full - acts_fs.astype(jnp.float32)
    gerr = err.astype(jnp.bfloat16)
    recon_fs = full.astype(jnp.bfloat16)
    recon = (
        lax.all_to_all(recon_fs.reshape(dp_count, tok_rows, fs), "dp", 0, 0, tiled=True)
        .transpose(1, 0, 2)
        .reshape(tok_rows, half)
    )
    grad_dec_bias = lax.all_gather(jnp.sum(err, axis=0), "dp", axis=0, tiled=True)

    gerr_slots = to_slots(gerr)
    gc_part = jnp.einsum("ocf,olf->ocl", gerr_slots, w_fs, preferred_element_type=jnp.float32)
    gcodes = lax.psum_scatter(slots_to_pairs(gc_part), ALL, scatter_dimension=0, tiled=True)
    gpre = gcodes * gate * (pre > 0.0).astype(jnp.float32)
    own_hit = (
        my_ids[:, :, None] == jnp.arange(owner_total, dtype=jnp.int32)[None, None, :]
    ).astype(jnp.float32)
    genc_part = jnp.sum(own_hit[:, :, :, None] * gpre[:, :, None, :], axis=(0, 1))
    grad_enc_bias = lax.psum_scatter(genc_part.reshape(-1), ALL, scatter_dimension=0, tiled=True)

    gpre_all = lax.all_gather(gpre.astype(jnp.bfloat16), ALL, axis=0, tiled=True)
    gpre_slots = pairs_to_slots(gpre_all)
    gw = jnp.einsum("ocl,ocf->olf", codes_slots, gerr_slots, preferred_element_type=jnp.float32)
    gw = gw + jnp.einsum(
        "ocl,ocf->olf", gpre_slots, acts_slots, preferred_element_type=jnp.float32
    )
    gw_back = lax.all_to_all(gw.astype(jnp.bfloat16), ALL, 0, 0, tiled=True)
    grad_weights = (
        gw_back.reshape(dp_count, lat_count, lat_own, fs)
        .transpose(2, 1, 0, 3)
        .reshape(lat_own, full_width)
    )
    return (recon, grad_weights, grad_enc_bias, grad_dec_bias)


def solution(mesh):
    in_specs = (
        P("dp", "lat"),
        P("dp", None),
        P("dp", None),
        P(("dp", "lat"), None),
        P(("dp", "lat")),
        P("lat"),
    )
    out_specs = (P("dp", "lat"), P(("dp", "lat"), None), P(("dp", "lat")), P("lat"))
    return jax.shard_map(local, mesh=mesh, in_specs=in_specs, out_specs=out_specs, check_vma=False)
```

```python
import jax
import jax.numpy as jnp
from jax import lax
from jax.sharding import PartitionSpec as P

BLK_DEV = 2
ALL = ("dp", "lat")
F32 = jnp.float32
BF16 = jnp.bfloat16


def slot_tables(ids, owner_total, block_rows, slot_cap):
    tokens, own_count = ids.shape
    blocks = tokens // block_rows
    onehot = (ids[:, :, None] == jnp.arange(owner_total, dtype=jnp.int32)[None, None, :]).astype(
        jnp.int32
    )
    present = jnp.sum(onehot, axis=1).reshape(blocks, block_rows, owner_total)
    before = (jnp.cumsum(present, axis=1) - present).reshape(tokens, owner_total)
    rank = jnp.take_along_axis(before, ids, axis=1)
    slot = ids * slot_cap + rank
    slots = owner_total * slot_cap
    sel = (slot[:, :, None] == jnp.arange(slots, dtype=jnp.int32)[None, None, :]).astype(BF16)
    sel = sel.reshape(blocks, block_rows, own_count, slots)
    place = jnp.sum(sel, axis=2)
    return sel, place


def split_hi_lo(x):
    hi = lax.reduce_precision(x, exponent_bits=8, mantissa_bits=7)
    return hi.astype(BF16), (x - hi).astype(BF16)


def local(acts, owner_ids, block_codes, weights, enc_bias, dec_bias):
    dp_count = lax.axis_size("dp")
    lat_count = lax.axis_size("lat")
    dp_idx = lax.axis_index("dp")
    lat_idx = lax.axis_index("lat")
    me = dp_idx * lat_count + lat_idx
    owner_total = dp_count * lat_count
    tok_rows, own_count = owner_ids.shape
    half = acts.shape[1]
    full_width = weights.shape[1]
    lat_own = weights.shape[0]
    block_width = lat_own // BLK_DEV
    fs = half // dp_count
    mine_rows = tok_rows // lat_count
    tokens = tok_rows * dp_count
    blocks = dp_count
    slot_cap = max(2, 2 * tok_rows * own_count // owner_total)

    def rs_tokens(x):
        tail = x.shape[1:]
        y = x.reshape((dp_count, lat_count, mine_rows) + tail).swapaxes(0, 1)
        y = lax.psum_scatter(y, "lat", scatter_dimension=0, tiled=True)[0]
        return lax.psum_scatter(y, "dp", scatter_dimension=0, tiled=True)[0]

    def ag_tokens(x):
        y = lax.all_gather(x, "dp", axis=0, tiled=False)
        y = lax.all_gather(y, "lat", axis=1, tiled=False)
        return y.reshape((tokens,) + x.shape[1:])

    acts_fs = lax.all_to_all(
        acts.reshape(tok_rows, dp_count, fs).transpose(1, 0, 2), "dp", 0, 0, tiled=True
    )
    w_send = (
        weights.reshape(lat_own, lat_count, dp_count, fs)
        .transpose(2, 1, 0, 3)
        .reshape(owner_total, lat_own, fs)
    )
    w_fs = lax.all_to_all(w_send, ALL, 0, 0, tiled=True)

    ids_all = lax.all_gather(owner_ids, "dp", axis=0, tiled=True)
    sel, place = slot_tables(ids_all, owner_total, tok_rows, slot_cap)

    def rows_to_slots(x_fs):
        y = jnp.einsum("btq,btf->bqf", place, x_fs, preferred_element_type=F32).astype(BF16)
        return y.reshape(blocks, owner_total, slot_cap, fs)

    def slots_to_pairs(v):
        v = v.reshape(blocks, owner_total * slot_cap, -1)
        width = v.shape[-1]
        both = jnp.concatenate(split_hi_lo(v), axis=-1)
        out = jnp.einsum("btkq,bql->btkl", sel, both, preferred_element_type=F32)
        out = out[..., :width] + out[..., width:]
        return out.reshape(tokens, own_count, width)

    def pairs_to_slots(x):
        x = x.reshape(blocks, tok_rows, own_count, -1)
        y = jnp.einsum("btkq,btkl->bql", sel, x, preferred_element_type=F32).astype(BF16)
        return y.reshape(blocks, owner_total, slot_cap, -1)

    acts_slots = rows_to_slots(acts_fs)
    pre_part = jnp.einsum("borf,olf->borl", acts_slots, w_fs, preferred_element_type=F32)
    own_bias = jnp.where(
        (jnp.arange(owner_total) == me)[:, None], enc_bias[None, :], 0.0
    )
    pre_part = pre_part + own_bias[None, :, None, :]
    pre = rs_tokens(slots_to_pairs(pre_part))

    start = lat_idx * mine_rows
    my_ids = lax.dynamic_slice_in_dim(owner_ids, start, mine_rows, 0)
    my_codes = lax.dynamic_slice_in_dim(block_codes, start, mine_rows, 0)
    lat_block = jnp.arange(lat_own, dtype=jnp.int32) // block_width
    gate = ((my_codes[:, :, None] // (2**lat_block)[None, None, :]) % 2).astype(F32)
    codes = (jnp.maximum(pre, 0.0) * gate).astype(BF16)

    codes_slots = pairs_to_slots(ag_tokens(codes))
    contrib = jnp.einsum("borl,olf->borf", codes_slots, w_fs, preferred_element_type=F32)
    contrib = contrib.astype(BF16).reshape(blocks, owner_total * slot_cap, fs)
    summed = jnp.einsum("btq,bqf->btf", place, contrib, preferred_element_type=F32)
    bias_fs = lax.dynamic_slice_in_dim(dec_bias, dp_idx * fs, fs, 0)
    full = summed + bias_fs[None, None, :]
    err = full - acts_fs.astype(F32)
    gerr = err.astype(BF16)
    recon = (
        lax.all_to_all(full.astype(BF16), "dp", 0, 0, tiled=True)
        .transpose(1, 0, 2)
        .reshape(tok_rows, half)
    )
    grad_dec_bias = lax.all_gather(jnp.sum(err, axis=(0, 1)), "dp", axis=0, tiled=True)

    gerr_slots = rows_to_slots(gerr)
    gc_part = jnp.einsum("borf,olf->borl", gerr_slots, w_fs, preferred_element_type=F32)
    gcodes = rs_tokens(slots_to_pairs(gc_part))
    gpre = gcodes * gate * (pre > 0.0).astype(F32)
    own_hit = (
        my_ids[:, :, None] == jnp.arange(owner_total, dtype=jnp.int32)[None, None, :]
    ).astype(F32)
    genc_part = jnp.sum(own_hit[:, :, :, None] * gpre[:, :, None, :], axis=(0, 1))
    grad_enc_bias = lax.psum_scatter(genc_part.reshape(-1), ALL, scatter_dimension=0, tiled=True)

    gpre_slots = pairs_to_slots(ag_tokens(gpre.astype(BF16)))
    gw = jnp.einsum("borl,borf->olf", codes_slots, gerr_slots, preferred_element_type=F32)
    gw = gw + jnp.einsum("borl,borf->olf", gpre_slots, acts_slots, preferred_element_type=F32)
    gw_back = lax.all_to_all(gw.astype(BF16), ALL, 0, 0, tiled=True)
    grad_weights = (
        gw_back.reshape(dp_count, lat_count, lat_own, fs)
        .transpose(2, 1, 0, 3)
        .reshape(lat_own, full_width)
    )
    return (recon, grad_weights, grad_enc_bias, grad_dec_bias)


def solution(mesh):
    in_specs = (
        P("dp", "lat"),
        P("dp", None),
        P("dp", None),
        P(("dp", "lat"), None),
        P(("dp", "lat")),
        P("lat"),
    )
    out_specs = (P("dp", "lat"), P(("dp", "lat"), None), P(("dp", "lat")), P("lat"))
    return jax.shard_map(local, mesh=mesh, in_specs=in_specs, out_specs=out_specs, check_vma=False)
```

```python
import jax
import jax.numpy as jnp
from jax import lax
from jax.sharding import PartitionSpec as P

BLK_DEV = 2
ALL = ("dp", "lat")
F32 = jnp.float32
BF16 = jnp.bfloat16


def slot_tables(ids, owner_total, block_rows, slot_cap):
    tokens, own_count = ids.shape
    blocks = tokens // block_rows
    onehot = (ids[:, :, None] == jnp.arange(owner_total, dtype=jnp.int32)[None, None, :]).astype(
        jnp.int32
    )
    present = jnp.sum(onehot, axis=1).reshape(blocks, block_rows, owner_total)
    before = (jnp.cumsum(present, axis=1) - present).reshape(tokens, owner_total)
    rank = jnp.sum(onehot * before[:, None, :], axis=2)
    slot = ids * slot_cap + rank
    slots = owner_total * slot_cap
    sel = (slot[:, :, None] == jnp.arange(slots, dtype=jnp.int32)[None, None, :]).astype(BF16)
    sel = sel.reshape(blocks, block_rows, own_count, slots)
    place = jnp.sum(sel, axis=2)
    return sel, place


def split_hi_lo(x):
    hi = lax.reduce_precision(x, exponent_bits=8, mantissa_bits=7)
    return hi.astype(BF16), (x - hi).astype(BF16)


def local(acts, owner_ids, block_codes, weights, enc_bias, dec_bias):
    dp_count = lax.axis_size("dp")
    lat_count = lax.axis_size("lat")
    dp_idx = lax.axis_index("dp")
    lat_idx = lax.axis_index("lat")
    me = dp_idx * lat_count + lat_idx
    owner_total = dp_count * lat_count
    tok_rows, own_count = owner_ids.shape
    half = acts.shape[1]
    full_width = weights.shape[1]
    lat_own = weights.shape[0]
    block_width = lat_own // BLK_DEV
    fs = half // dp_count
    mine_rows = tok_rows // lat_count
    tokens = tok_rows * dp_count
    blocks = dp_count
    slot_cap = max(2, 2 * tok_rows * own_count // owner_total)

    def rs_tokens(x):
        tail = x.shape[1:]
        y = x.reshape((dp_count, lat_count, mine_rows) + tail).swapaxes(0, 1)
        y = jnp.sum(lax.all_to_all(y, "lat", 0, 0, tiled=True), axis=0)
        return jnp.sum(lax.all_to_all(y, "dp", 0, 0, tiled=True), axis=0)

    def ag_tokens(x):
        y = lax.all_to_all(jnp.broadcast_to(x[None], (dp_count,) + x.shape), "dp", 0, 0, tiled=True)
        y = lax.all_gather(y, "lat", axis=1, tiled=False)
        return y.reshape((tokens,) + x.shape[1:])

    acts_fs = lax.all_to_all(
        acts.reshape(tok_rows, dp_count, fs).transpose(1, 0, 2), "dp", 0, 0, tiled=True
    )
    w_send = (
        weights.reshape(lat_own, lat_count, dp_count, fs)
        .transpose(2, 1, 0, 3)
        .reshape(owner_total, lat_own, fs)
    )
    w_fs = lax.all_to_all(w_send, ALL, 0, 0, tiled=True)

    ids_rep = jnp.broadcast_to(owner_ids.astype(F32)[None], (dp_count, tok_rows, own_count))
    ids_all = lax.all_to_all(ids_rep, "dp", 0, 0, tiled=True).astype(jnp.int32)
    ids_all = ids_all.reshape(tokens, own_count)
    sel, place = slot_tables(ids_all, owner_total, tok_rows, slot_cap)

    def rows_to_slots(x_fs):
        y = jnp.einsum("btq,btf->bqf", place, x_fs, preferred_element_type=F32).astype(BF16)
        return y.reshape(blocks, owner_total, slot_cap, fs)

    def slots_to_pairs(v):
        v = v.reshape(blocks, owner_total * slot_cap, -1)
        width = v.shape[-1]
        both = jnp.concatenate(split_hi_lo(v), axis=-1)
        out = jnp.einsum("btkq,bql->btkl", sel, both, preferred_element_type=F32)
        out = out[..., :width] + out[..., width:]
        return out.reshape(tokens, own_count, width)

    def pairs_to_slots(x):
        x = x.reshape(blocks, tok_rows, own_count, -1)
        y = jnp.einsum("btkq,btkl->bql", sel, x, preferred_element_type=F32).astype(BF16)
        return y.reshape(blocks, owner_total, slot_cap, -1)

    acts_slots = rows_to_slots(acts_fs)
    pre_part = jnp.einsum("borf,olf->borl", acts_slots, w_fs, preferred_element_type=F32)
    own_bias = jnp.where(
        (jnp.arange(owner_total) == me)[:, None], enc_bias[None, :], 0.0
    )
    pre_part = pre_part + own_bias[None, :, None, :]
    pre = rs_tokens(slots_to_pairs(pre_part))

    start = lat_idx * mine_rows
    my_ids = lax.dynamic_slice_in_dim(owner_ids, start, mine_rows, 0)
    my_codes = lax.dynamic_slice_in_dim(block_codes, start, mine_rows, 0)
    lat_block = jnp.arange(lat_own, dtype=jnp.int32) // block_width
    gate = ((my_codes[:, :, None] // (2**lat_block)[None, None, :]) % 2).astype(F32)
    codes = (jnp.maximum(pre, 0.0) * gate).astype(BF16)

    codes_slots = pairs_to_slots(ag_tokens(codes))
    contrib = jnp.einsum("borl,olf->borf", codes_slots, w_fs, preferred_element_type=F32)
    contrib = contrib.astype(BF16).reshape(blocks, owner_total * slot_cap, fs)
    summed = jnp.einsum("btq,bqf->btf", place, contrib, preferred_element_type=F32)
    bias_fs = lax.dynamic_slice_in_dim(dec_bias, dp_idx * fs, fs, 0)
    full = summed + bias_fs[None, None, :]
    err = full - acts_fs.astype(F32)
    gerr = err.astype(BF16)
    recon = (
        lax.all_to_all(full.astype(BF16), "dp", 0, 0, tiled=True)
        .transpose(1, 0, 2)
        .reshape(tok_rows, half)
    )
    gdb_rep = jnp.broadcast_to(jnp.sum(err, axis=(0, 1))[None], (dp_count, fs))
    grad_dec_bias = lax.all_to_all(gdb_rep, "dp", 0, 0, tiled=True).reshape(half)

    gerr_slots = rows_to_slots(gerr)
    gc_part = jnp.einsum("borf,olf->borl", gerr_slots, w_fs, preferred_element_type=F32)
    gcodes = rs_tokens(slots_to_pairs(gc_part))
    gpre = gcodes * gate * (pre > 0.0).astype(F32)
    own_hit = (
        my_ids[:, :, None] == jnp.arange(owner_total, dtype=jnp.int32)[None, None, :]
    ).astype(F32)
    genc_part = jnp.sum(own_hit[:, :, :, None] * gpre[:, :, None, :], axis=(0, 1))
    grad_enc_bias = jnp.sum(lax.all_to_all(genc_part, ALL, 0, 0, tiled=True), axis=0)

    gpre_slots = pairs_to_slots(ag_tokens(gpre.astype(BF16)))
    gw = jnp.einsum("borl,borf->olf", codes_slots, gerr_slots, preferred_element_type=F32)
    gw = gw + jnp.einsum("borl,borf->olf", gpre_slots, acts_slots, preferred_element_type=F32)
    gw_back = lax.all_to_all(gw.astype(BF16), ALL, 0, 0, tiled=True)
    grad_weights = (
        gw_back.reshape(dp_count, lat_count, lat_own, fs)
        .transpose(2, 1, 0, 3)
        .reshape(lat_own, full_width)
    )
    return (recon, grad_weights, grad_enc_bias, grad_dec_bias)


def solution(mesh):
    in_specs = (
        P("dp", "lat"),
        P("dp", None),
        P("dp", None),
        P(("dp", "lat"), None),
        P(("dp", "lat")),
        P("lat"),
    )
    out_specs = (P("dp", "lat"), P(("dp", "lat"), None), P(("dp", "lat")), P("lat"))
    return jax.shard_map(local, mesh=mesh, in_specs=in_specs, out_specs=out_specs, check_vma=False)
```

```python
import jax
import jax.numpy as jnp
from jax import lax
from jax.sharding import PartitionSpec as P

BLK_DEV = 2
ALL = ("dp", "lat")
F32 = jnp.float32
BF16 = jnp.bfloat16


def slot_tables(ids, owner_total, block_rows, slot_cap):
    tokens, own_count = ids.shape
    blocks = tokens // block_rows
    onehot = (ids[:, :, None] == jnp.arange(owner_total, dtype=jnp.int32)[None, None, :]).astype(
        jnp.int32
    )
    present = jnp.sum(onehot, axis=1).reshape(blocks, block_rows, owner_total)
    before = (jnp.cumsum(present, axis=1) - present).reshape(tokens, owner_total)
    rank = jnp.sum(onehot * before[:, None, :], axis=2)
    slot = ids * slot_cap + rank
    slots = owner_total * slot_cap
    sel = (slot[:, :, None] == jnp.arange(slots, dtype=jnp.int32)[None, None, :]).astype(BF16)
    sel = sel.reshape(blocks, block_rows, own_count, slots)
    place = jnp.sum(sel, axis=2)
    return sel, place


def split_hi_lo(x):
    hi = lax.reduce_precision(x, exponent_bits=8, mantissa_bits=7)
    return hi.astype(BF16), (x - hi).astype(BF16)


def local(acts, owner_ids, block_codes, weights, enc_bias, dec_bias):
    dp_count = lax.axis_size("dp")
    lat_count = lax.axis_size("lat")
    dp_idx = lax.axis_index("dp")
    lat_idx = lax.axis_index("lat")
    me = dp_idx * lat_count + lat_idx
    owner_total = dp_count * lat_count
    tok_rows, own_count = owner_ids.shape
    half = acts.shape[1]
    full_width = weights.shape[1]
    lat_own = weights.shape[0]
    block_width = lat_own // BLK_DEV
    fs = half // dp_count
    mine_rows = tok_rows // lat_count
    tokens = tok_rows * dp_count
    blocks = dp_count
    slot_cap = max(2, 2 * tok_rows * own_count // owner_total)

    def rs_tokens(x):
        tail = x.shape[1:]
        y = x.reshape((dp_count, lat_count, mine_rows) + tail).swapaxes(0, 1)
        y = jnp.sum(lax.all_to_all(y, "lat", 0, 0, tiled=True), axis=0)
        return jnp.sum(lax.all_to_all(y, "dp", 0, 0, tiled=True), axis=0)

    def ag_tokens(x):
        y = lax.all_to_all(jnp.broadcast_to(x[None], (dp_count,) + x.shape), "dp", 0, 0, tiled=True)
        y = lax.all_gather(y, "lat", axis=1, tiled=False)
        return y.reshape((tokens,) + x.shape[1:])

    id_vals = tok_rows * own_count * 2
    id_rows = -(-id_vals // fs)
    id_code = jnp.concatenate([owner_ids // 16, owner_ids % 16], axis=1).astype(BF16).reshape(-1)
    id_code = jnp.pad(id_code, (0, id_rows * fs - id_vals)).reshape(id_rows, fs)
    acts_send = jnp.concatenate(
        [
            acts.reshape(tok_rows, dp_count, fs).transpose(1, 0, 2),
            jnp.broadcast_to(id_code[None], (dp_count, id_rows, fs)),
        ],
        axis=1,
    )
    acts_got = lax.all_to_all(acts_send, "dp", 0, 0, tiled=True)
    acts_fs = acts_got[:, :tok_rows]
    id_got = acts_got[:, tok_rows:].reshape(dp_count, id_rows * fs)[:, :id_vals]
    id_got = id_got.astype(jnp.int32).reshape(dp_count, tok_rows, 2, own_count)
    ids_all = (id_got[:, :, 0] * 16 + id_got[:, :, 1]).reshape(tokens, own_count)
    w_send = (
        weights.reshape(lat_own, lat_count, dp_count, fs)
        .transpose(2, 1, 0, 3)
        .reshape(owner_total, lat_own, fs)
    )
    w_fs = lax.all_to_all(w_send, ALL, 0, 0, tiled=True)

    sel, place = slot_tables(ids_all, owner_total, tok_rows, slot_cap)

    def rows_to_slots(x_fs):
        y = jnp.einsum("btq,btf->bqf", place, x_fs, preferred_element_type=F32).astype(BF16)
        return y.reshape(blocks, owner_total, slot_cap, fs)

    def slots_to_pairs(v):
        v = v.reshape(blocks, owner_total * slot_cap, -1)
        width = v.shape[-1]
        both = jnp.concatenate(split_hi_lo(v), axis=-1)
        out = jnp.einsum("btkq,bql->btkl", sel, both, preferred_element_type=F32)
        out = out[..., :width] + out[..., width:]
        return out.reshape(tokens, own_count, width)

    def pairs_to_slots(x):
        x = x.reshape(blocks, tok_rows, own_count, -1)
        y = jnp.einsum("btkq,btkl->bql", sel, x, preferred_element_type=F32).astype(BF16)
        return y.reshape(blocks, owner_total, slot_cap, -1)

    acts_slots = rows_to_slots(acts_fs)
    pre_part = jnp.einsum("borf,olf->borl", acts_slots, w_fs, preferred_element_type=F32)
    own_bias = jnp.where(
        (jnp.arange(owner_total) == me)[:, None], enc_bias[None, :], 0.0
    )
    pre_part = pre_part + own_bias[None, :, None, :]
    pre = rs_tokens(slots_to_pairs(pre_part))

    start = lat_idx * mine_rows
    my_ids = lax.dynamic_slice_in_dim(owner_ids, start, mine_rows, 0)
    my_codes = lax.dynamic_slice_in_dim(block_codes, start, mine_rows, 0)
    lat_block = jnp.arange(lat_own, dtype=jnp.int32) // block_width
    gate = ((my_codes[:, :, None] // (2**lat_block)[None, None, :]) % 2).astype(F32)
    codes = (jnp.maximum(pre, 0.0) * gate).astype(BF16)

    codes_slots = pairs_to_slots(ag_tokens(codes))
    contrib = jnp.einsum("borl,olf->borf", codes_slots, w_fs, preferred_element_type=F32)
    contrib = contrib.astype(BF16).reshape(blocks, owner_total * slot_cap, fs)
    summed = jnp.einsum("btq,bqf->btf", place, contrib, preferred_element_type=F32)
    bias_fs = lax.dynamic_slice_in_dim(dec_bias, dp_idx * fs, fs, 0)
    full = summed + bias_fs[None, None, :]
    err = full - acts_fs.astype(F32)
    gerr = err.astype(BF16)
    gdb = jnp.stack(split_hi_lo(jnp.sum(err, axis=(0, 1))))
    recon_send = jnp.concatenate(
        [full.astype(BF16), jnp.broadcast_to(gdb[None], (dp_count, 2, fs))], axis=1
    )
    recon_got = lax.all_to_all(recon_send, "dp", 0, 0, tiled=True)
    recon = recon_got[:, :tok_rows].transpose(1, 0, 2).reshape(tok_rows, half)
    gdb_got = recon_got[:, tok_rows:].astype(F32)
    grad_dec_bias = (gdb_got[:, 0] + gdb_got[:, 1]).reshape(half)

    gerr_slots = rows_to_slots(gerr)
    gc_part = jnp.einsum("borf,olf->borl", gerr_slots, w_fs, preferred_element_type=F32)
    gcodes = rs_tokens(slots_to_pairs(gc_part))
    gpre = gcodes * gate * (pre > 0.0).astype(F32)
    own_hit = (
        my_ids[:, :, None] == jnp.arange(owner_total, dtype=jnp.int32)[None, None, :]
    ).astype(F32)
    genc_part = jnp.sum(own_hit[:, :, :, None] * gpre[:, :, None, :], axis=(0, 1))

    gpre_slots = pairs_to_slots(ag_tokens(gpre.astype(BF16)))
    gw = jnp.einsum("borl,borf->olf", codes_slots, gerr_slots, preferred_element_type=F32)
    gw = gw + jnp.einsum("borl,borf->olf", gpre_slots, acts_slots, preferred_element_type=F32)
    enc_vals = 2 * lat_own
    enc_rows = -(-enc_vals // fs)
    genc = jnp.concatenate(split_hi_lo(genc_part), axis=1)
    genc = jnp.pad(genc, ((0, 0), (0, enc_rows * fs - enc_vals))).reshape(owner_total, enc_rows, fs)
    gw_got = lax.all_to_all(
        jnp.concatenate([gw.astype(BF16), genc], axis=1), ALL, 0, 0, tiled=True
    )
    gw_back = gw_got[:, :lat_own]
    genc_got = gw_got[:, lat_own:].reshape(owner_total, enc_rows * fs)[:, :enc_vals].astype(F32)
    grad_enc_bias = jnp.sum(genc_got[:, :lat_own] + genc_got[:, lat_own:], axis=0)
    grad_weights = (
        gw_back.reshape(dp_count, lat_count, lat_own, fs)
        .transpose(2, 1, 0, 3)
        .reshape(lat_own, full_width)
    )
    return (recon, grad_weights, grad_enc_bias, grad_dec_bias)


def solution(mesh):
    in_specs = (
        P("dp", "lat"),
        P("dp", None),
        P("dp", None),
        P(("dp", "lat"), None),
        P(("dp", "lat")),
        P("lat"),
    )
    out_specs = (P("dp", "lat"), P(("dp", "lat"), None), P(("dp", "lat")), P("lat"))
    return jax.shard_map(local, mesh=mesh, in_specs=in_specs, out_specs=out_specs, check_vma=False)
```

```python
import jax
import jax.numpy as jnp
from jax import lax
from jax.sharding import PartitionSpec as P

BLK_DEV = 2
ALL = ("dp", "lat")
F32 = jnp.float32
BF16 = jnp.bfloat16


def slot_tables(ids, owner_total, block_rows, slot_cap):
    tokens, own_count = ids.shape
    blocks = tokens // block_rows
    onehot = (ids[:, :, None] == jnp.arange(owner_total, dtype=jnp.int32)[None, None, :]).astype(
        jnp.int32
    )
    present = jnp.sum(onehot, axis=1).reshape(blocks, block_rows, owner_total)
    before = (jnp.cumsum(present, axis=1) - present).reshape(tokens, owner_total)
    rank = jnp.sum(onehot * before[:, None, :], axis=2)
    slot = ids * slot_cap + rank
    slots = owner_total * slot_cap
    sel = (slot[:, :, None] == jnp.arange(slots, dtype=jnp.int32)[None, None, :]).astype(BF16)
    sel = sel.reshape(blocks, block_rows, own_count, slots)
    place = jnp.sum(sel, axis=2)
    return sel, place


def split_hi_lo(x):
    hi = lax.reduce_precision(x, exponent_bits=8, mantissa_bits=7)
    return hi.astype(BF16), (x - hi).astype(BF16)


def local(acts, owner_ids, block_codes, weights, enc_bias, dec_bias):
    dp_count = lax.axis_size("dp")
    lat_count = lax.axis_size("lat")
    dp_idx = lax.axis_index("dp")
    lat_idx = lax.axis_index("lat")
    me = dp_idx * lat_count + lat_idx
    owner_total = dp_count * lat_count
    tok_rows, own_count = owner_ids.shape
    half = acts.shape[1]
    full_width = weights.shape[1]
    lat_own = weights.shape[0]
    block_width = lat_own // BLK_DEV
    fs = half // dp_count
    mine_rows = tok_rows // lat_count
    tokens = tok_rows * dp_count
    blocks = dp_count
    slot_cap = max(2, 2 * tok_rows * own_count // owner_total)

    def rs_tokens(x):
        tail = x.shape[1:]
        y = x.reshape((dp_count, lat_count, mine_rows) + tail).swapaxes(0, 1)
        y = jnp.sum(lax.all_to_all(y, "lat", 0, 0, tiled=True), axis=0)
        return jnp.sum(lax.all_to_all(y, "dp", 0, 0, tiled=True), axis=0)

    def ag_tokens(x):
        y = lax.all_to_all(jnp.broadcast_to(x[None], (dp_count,) + x.shape), "dp", 0, 0, tiled=True)
        y = lax.all_gather(y, "lat", axis=1, tiled=False)
        return y.reshape((tokens,) + x.shape[1:])

    id_vals = tok_rows * own_count * 2
    id_rows = -(-id_vals // fs)
    id_code = jnp.concatenate([owner_ids // 16, owner_ids % 16], axis=1).astype(BF16).reshape(-1)
    id_code = jnp.pad(id_code, (0, id_rows * fs - id_vals)).reshape(id_rows, fs)
    w_dp = (
        weights.reshape(lat_own, lat_count, dp_count, fs)
        .transpose(2, 1, 0, 3)
        .reshape(dp_count, lat_count * lat_own, fs)
    )
    acts_send = jnp.concatenate(
        [
            acts.reshape(tok_rows, dp_count, fs).transpose(1, 0, 2),
            jnp.broadcast_to(id_code[None], (dp_count, id_rows, fs)),
            w_dp,
        ],
        axis=1,
    )
    acts_got = lax.all_to_all(acts_send, "dp", 0, 0, tiled=True)
    acts_fs = acts_got[:, :tok_rows]
    w_got = acts_got[:, tok_rows + id_rows :].reshape(dp_count, lat_count, lat_own, fs)
    w_got = lax.all_to_all(w_got.transpose(1, 0, 2, 3), "lat", 0, 0, tiled=True)
    w_fs = w_got.transpose(1, 0, 2, 3).reshape(owner_total, lat_own, fs)
    id_got = acts_got[:, tok_rows : tok_rows + id_rows].reshape(dp_count, id_rows * fs)[:, :id_vals]
    id_got = id_got.astype(jnp.int32).reshape(dp_count, tok_rows, 2, own_count)
    ids_all = (id_got[:, :, 0] * 16 + id_got[:, :, 1]).reshape(tokens, own_count)

    sel, place = slot_tables(ids_all, owner_total, tok_rows, slot_cap)

    def rows_to_slots(x_fs):
        y = jnp.einsum("btq,btf->bqf", place, x_fs, preferred_element_type=F32).astype(BF16)
        return y.reshape(blocks, owner_total, slot_cap, fs)

    def slots_to_pairs(v):
        v = v.reshape(blocks, owner_total * slot_cap, -1)
        width = v.shape[-1]
        both = jnp.concatenate(split_hi_lo(v), axis=-1)
        out = jnp.einsum("btkq,bql->btkl", sel, both, preferred_element_type=F32)
        out = out[..., :width] + out[..., width:]
        return out.reshape(tokens, own_count, width)

    def pairs_to_slots(x):
        x = x.reshape(blocks, tok_rows, own_count, -1)
        y = jnp.einsum("btkq,btkl->bql", sel, x, preferred_element_type=F32).astype(BF16)
        return y.reshape(blocks, owner_total, slot_cap, -1)

    acts_slots = rows_to_slots(acts_fs)
    pre_part = jnp.einsum("borf,olf->borl", acts_slots, w_fs, preferred_element_type=F32)
    own_bias = jnp.where(
        (jnp.arange(owner_total) == me)[:, None], enc_bias[None, :], 0.0
    )
    pre_part = pre_part + own_bias[None, :, None, :]
    pre = rs_tokens(slots_to_pairs(pre_part))

    start = lat_idx * mine_rows
    my_ids = lax.dynamic_slice_in_dim(owner_ids, start, mine_rows, 0)
    my_codes = lax.dynamic_slice_in_dim(block_codes, start, mine_rows, 0)
    lat_block = jnp.arange(lat_own, dtype=jnp.int32) // block_width
    gate = ((my_codes[:, :, None] // (2**lat_block)[None, None, :]) % 2).astype(F32)
    codes = (jnp.maximum(pre, 0.0) * gate).astype(BF16)

    codes_slots = pairs_to_slots(ag_tokens(codes))
    contrib = jnp.einsum("borl,olf->borf", codes_slots, w_fs, preferred_element_type=F32)
    contrib = contrib.astype(BF16).reshape(blocks, owner_total * slot_cap, fs)
    summed = jnp.einsum("btq,bqf->btf", place, contrib, preferred_element_type=F32)
    bias_fs = lax.dynamic_slice_in_dim(dec_bias, dp_idx * fs, fs, 0)
    full = summed + bias_fs[None, None, :]
    err = full - acts_fs.astype(F32)
    gerr = err.astype(BF16)
    gdb = jnp.stack(split_hi_lo(jnp.sum(err, axis=(0, 1))))
    recon_send = jnp.concatenate(
        [full.astype(BF16), jnp.broadcast_to(gdb[None], (dp_count, 2, fs))], axis=1
    )
    recon_got = lax.all_to_all(recon_send, "dp", 0, 0, tiled=True)
    recon = recon_got[:, :tok_rows].transpose(1, 0, 2).reshape(tok_rows, half)
    gdb_got = recon_got[:, tok_rows:].astype(F32)
    grad_dec_bias = (gdb_got[:, 0] + gdb_got[:, 1]).reshape(half)

    gerr_slots = rows_to_slots(gerr)
    gc_part = jnp.einsum("borf,olf->borl", gerr_slots, w_fs, preferred_element_type=F32)
    gcodes = rs_tokens(slots_to_pairs(gc_part))
    gpre = gcodes * gate * (pre > 0.0).astype(F32)
    own_hit = (
        my_ids[:, :, None] == jnp.arange(owner_total, dtype=jnp.int32)[None, None, :]
    ).astype(F32)
    genc_part = jnp.sum(own_hit[:, :, :, None] * gpre[:, :, None, :], axis=(0, 1))

    gpre_slots = pairs_to_slots(ag_tokens(gpre.astype(BF16)))
    gw = jnp.einsum("borl,borf->olf", codes_slots, gerr_slots, preferred_element_type=F32)
    gw = gw + jnp.einsum("borl,borf->olf", gpre_slots, acts_slots, preferred_element_type=F32)
    enc_vals = 2 * lat_own
    enc_rows = -(-enc_vals // fs)
    genc = jnp.concatenate(split_hi_lo(genc_part), axis=1)
    genc = jnp.pad(genc, ((0, 0), (0, enc_rows * fs - enc_vals))).reshape(owner_total, enc_rows, fs)
    gw_got = lax.all_to_all(
        jnp.concatenate([gw.astype(BF16), genc], axis=1), ALL, 0, 0, tiled=True
    )
    gw_back = gw_got[:, :lat_own]
    genc_got = gw_got[:, lat_own:].reshape(owner_total, enc_rows * fs)[:, :enc_vals].astype(F32)
    grad_enc_bias = jnp.sum(genc_got[:, :lat_own] + genc_got[:, lat_own:], axis=0)
    grad_weights = (
        gw_back.reshape(dp_count, lat_count, lat_own, fs)
        .transpose(2, 1, 0, 3)
        .reshape(lat_own, full_width)
    )
    return (recon, grad_weights, grad_enc_bias, grad_dec_bias)


def solution(mesh):
    in_specs = (
        P("dp", "lat"),
        P("dp", None),
        P("dp", None),
        P(("dp", "lat"), None),
        P(("dp", "lat")),
        P("lat"),
    )
    out_specs = (P("dp", "lat"), P(("dp", "lat"), None), P(("dp", "lat")), P("lat"))
    return jax.shard_map(local, mesh=mesh, in_specs=in_specs, out_specs=out_specs, check_vma=False)
```

```python
import jax
import jax.numpy as jnp
from jax import lax
from jax.sharding import Mesh, PartitionSpec as P

BLK_DEV = 2
DP = ("dh", "dl")
ALL = ("dh", "dl", "lat")
F32 = jnp.float32
BF16 = jnp.bfloat16


def slot_tables(ids, owner_total, block_rows, slot_cap):
    tokens, own_count = ids.shape
    blocks = tokens // block_rows
    onehot = (ids[:, :, None] == jnp.arange(owner_total, dtype=jnp.int32)[None, None, :]).astype(
        jnp.int32
    )
    present = jnp.sum(onehot, axis=1).reshape(blocks, block_rows, owner_total)
    before = (jnp.cumsum(present, axis=1) - present).reshape(tokens, owner_total)
    rank = jnp.sum(onehot * before[:, None, :], axis=2)
    slot = ids * slot_cap + rank
    slots = owner_total * slot_cap
    sel = (slot[:, :, None] == jnp.arange(slots, dtype=jnp.int32)[None, None, :]).astype(BF16)
    sel = sel.reshape(blocks, block_rows, own_count, slots)
    place = jnp.sum(sel, axis=2)
    return sel, place


def split_hi_lo(x):
    hi = lax.reduce_precision(x, exponent_bits=8, mantissa_bits=7)
    return hi.astype(BF16), (x - hi).astype(BF16)


def local(acts, owner_ids, block_codes, weights, enc_bias, dec_bias):
    dp_count = lax.axis_size(DP)
    dh_count = lax.axis_size("dh")
    dl_count = lax.axis_size("dl")
    lat_count = lax.axis_size("lat")
    dp_idx = lax.axis_index("dh") * dl_count + lax.axis_index("dl")
    lat_idx = lax.axis_index("lat")
    me = dp_idx * lat_count + lat_idx
    owner_total = dp_count * lat_count
    tok_rows, own_count = owner_ids.shape
    half = acts.shape[1]
    full_width = weights.shape[1]
    lat_own = weights.shape[0]
    block_width = lat_own // BLK_DEV
    fs = half // dp_count
    mine_rows = tok_rows // lat_count
    tokens = tok_rows * dp_count
    blocks = dp_count
    slot_cap = max(2, 2 * tok_rows * own_count // owner_total)

    def rs_tokens(x):
        tail = x.shape[1:]
        y = x.reshape((dp_count, lat_count, mine_rows) + tail).swapaxes(0, 1)
        y = jnp.sum(lax.all_to_all(y, "lat", 0, 0, tiled=True), axis=0)
        y = y.reshape((dh_count, dl_count) + y.shape[1:]).swapaxes(0, 1)
        y = jnp.sum(lax.all_to_all(y, "dl", 0, 0, tiled=True), axis=0)
        return jnp.sum(lax.all_to_all(y, "dh", 0, 0, tiled=True), axis=0)

    def ag_tokens(x):
        y = lax.all_to_all(jnp.broadcast_to(x[None], (dh_count,) + x.shape), "dh", 0, 0, tiled=True)
        y = lax.all_to_all(
            jnp.broadcast_to(y[None], (dl_count,) + y.shape), "dl", 0, 0, tiled=True
        ).swapaxes(0, 1)
        y = y.reshape((dp_count,) + x.shape)
        y = lax.all_gather(y, "lat", axis=1, tiled=False)
        return y.reshape((tokens,) + x.shape[1:])

    id_vals = tok_rows * own_count * 2
    id_rows = -(-id_vals // fs)
    id_code = jnp.concatenate([owner_ids // 16, owner_ids % 16], axis=1).astype(BF16).reshape(-1)
    id_code = jnp.pad(id_code, (0, id_rows * fs - id_vals)).reshape(id_rows, fs)
    acts_send = jnp.concatenate(
        [
            acts.reshape(tok_rows, dp_count, fs).transpose(1, 0, 2),
            jnp.broadcast_to(id_code[None], (dp_count, id_rows, fs)),
        ],
        axis=1,
    )
    acts_got = lax.all_to_all(acts_send, DP, 0, 0, tiled=True)
    acts_fs = acts_got[:, :tok_rows]
    id_got = acts_got[:, tok_rows:].reshape(dp_count, id_rows * fs)[:, :id_vals]
    id_got = id_got.astype(jnp.int32).reshape(dp_count, tok_rows, 2, own_count)
    ids_all = (id_got[:, :, 0] * 16 + id_got[:, :, 1]).reshape(tokens, own_count)
    w_send = (
        weights.reshape(lat_own, lat_count, dp_count, fs)
        .transpose(2, 1, 0, 3)
        .reshape(owner_total, lat_own, fs)
    )
    w_fs = lax.all_to_all(w_send, ALL, 0, 0, tiled=True)

    sel, place = slot_tables(ids_all, owner_total, tok_rows, slot_cap)

    def rows_to_slots(x_fs):
        y = jnp.einsum("btq,btf->bqf", place, x_fs, preferred_element_type=F32).astype(BF16)
        return y.reshape(blocks, owner_total, slot_cap, fs)

    def slots_to_pairs(v):
        v = v.reshape(blocks, owner_total * slot_cap, -1)
        width = v.shape[-1]
        both = jnp.concatenate(split_hi_lo(v), axis=-1)
        out = jnp.einsum("btkq,bql->btkl", sel, both, preferred_element_type=F32)
        out = out[..., :width] + out[..., width:]
        return out.reshape(tokens, own_count, width)

    def pairs_to_slots(x):
        x = x.reshape(blocks, tok_rows, own_count, -1)
        y = jnp.einsum("btkq,btkl->bql", sel, x, preferred_element_type=F32).astype(BF16)
        return y.reshape(blocks, owner_total, slot_cap, -1)

    acts_slots = rows_to_slots(acts_fs)
    pre_part = jnp.einsum("borf,olf->borl", acts_slots, w_fs, preferred_element_type=F32)
    own_bias = jnp.where(
        (jnp.arange(owner_total) == me)[:, None], enc_bias[None, :], 0.0
    )
    pre_part = pre_part + own_bias[None, :, None, :]
    pre = rs_tokens(slots_to_pairs(pre_part))

    start = lat_idx * mine_rows
    my_ids = lax.dynamic_slice_in_dim(owner_ids, start, mine_rows, 0)
    my_codes = lax.dynamic_slice_in_dim(block_codes, start, mine_rows, 0)
    lat_block = jnp.arange(lat_own, dtype=jnp.int32) // block_width
    gate = ((my_codes[:, :, None] // (2**lat_block)[None, None, :]) % 2).astype(F32)
    codes = (jnp.maximum(pre, 0.0) * gate).astype(BF16)

    codes_slots = pairs_to_slots(ag_tokens(codes))
    contrib = jnp.einsum("borl,olf->borf", codes_slots, w_fs, preferred_element_type=F32)
    contrib = contrib.astype(BF16).reshape(blocks, owner_total * slot_cap, fs)
    summed = jnp.einsum("btq,bqf->btf", place, contrib, preferred_element_type=F32)
    bias_fs = lax.dynamic_slice_in_dim(dec_bias, dp_idx * fs, fs, 0)
    full = summed + bias_fs[None, None, :]
    err = full - acts_fs.astype(F32)
    gerr = err.astype(BF16)
    gdb = jnp.stack(split_hi_lo(jnp.sum(err, axis=(0, 1))))
    recon_send = jnp.concatenate(
        [full.astype(BF16), jnp.broadcast_to(gdb[None], (dp_count, 2, fs))], axis=1
    )
    recon_got = lax.all_to_all(recon_send, DP, 0, 0, tiled=True)
    recon = recon_got[:, :tok_rows].transpose(1, 0, 2).reshape(tok_rows, half)
    gdb_got = recon_got[:, tok_rows:].astype(F32)
    grad_dec_bias = (gdb_got[:, 0] + gdb_got[:, 1]).reshape(half)

    gerr_slots = rows_to_slots(gerr)
    gc_part = jnp.einsum("borf,olf->borl", gerr_slots, w_fs, preferred_element_type=F32)
    gcodes = rs_tokens(slots_to_pairs(gc_part))
    gpre = gcodes * gate * (pre > 0.0).astype(F32)
    own_hit = (
        my_ids[:, :, None] == jnp.arange(owner_total, dtype=jnp.int32)[None, None, :]
    ).astype(F32)
    genc_part = jnp.sum(own_hit[:, :, :, None] * gpre[:, :, None, :], axis=(0, 1))

    gpre_slots = pairs_to_slots(ag_tokens(gpre.astype(BF16)))
    gw = jnp.einsum("borl,borf->olf", codes_slots, gerr_slots, preferred_element_type=F32)
    gw = gw + jnp.einsum("borl,borf->olf", gpre_slots, acts_slots, preferred_element_type=F32)
    enc_vals = 2 * lat_own
    enc_rows = -(-enc_vals // fs)
    genc = jnp.concatenate(split_hi_lo(genc_part), axis=1)
    genc = jnp.pad(genc, ((0, 0), (0, enc_rows * fs - enc_vals))).reshape(owner_total, enc_rows, fs)
    gw_got = lax.all_to_all(
        jnp.concatenate([gw.astype(BF16), genc], axis=1), ALL, 0, 0, tiled=True
    )
    gw_back = gw_got[:, :lat_own]
    genc_got = gw_got[:, lat_own:].reshape(owner_total, enc_rows * fs)[:, :enc_vals].astype(F32)
    grad_enc_bias = jnp.sum(genc_got[:, :lat_own] + genc_got[:, lat_own:], axis=0)
    grad_weights = (
        gw_back.reshape(dp_count, lat_count, lat_own, fs)
        .transpose(2, 1, 0, 3)
        .reshape(lat_own, full_width)
    )
    return (recon, grad_weights, grad_enc_bias, grad_dec_bias)


def solution(mesh):
    dp_count, lat_count = mesh.devices.shape
    halves = 2 if dp_count % 2 == 0 else 1
    split = Mesh(mesh.devices.reshape(halves, dp_count // halves, lat_count), ("dh", "dl", "lat"))
    in_specs = (
        P(DP, "lat"),
        P(DP, None),
        P(DP, None),
        P(ALL, None),
        P(ALL),
        P("lat"),
    )
    out_specs = (P(DP, "lat"), P(ALL, None), P(ALL), P("lat"))
    return jax.shard_map(local, mesh=split, in_specs=in_specs, out_specs=out_specs, check_vma=False)
```

```python
import jax
import jax.numpy as jnp
from jax import lax
from jax.sharding import Mesh, PartitionSpec as P

BLK_DEV = 2
DP = ("dh", "dm", "dn")
ALL = ("dh", "dm", "dn", "lat")
F32 = jnp.float32
BF16 = jnp.bfloat16


def slot_tables(ids, owner_total, block_rows, slot_cap):
    tokens, own_count = ids.shape
    blocks = tokens // block_rows
    onehot = (ids[:, :, None] == jnp.arange(owner_total, dtype=jnp.int32)[None, None, :]).astype(
        jnp.int32
    )
    present = jnp.sum(onehot, axis=1).reshape(blocks, block_rows, owner_total)
    before = (jnp.cumsum(present, axis=1) - present).reshape(tokens, owner_total)
    rank = jnp.sum(onehot * before[:, None, :], axis=2)
    slot = ids * slot_cap + rank
    slots = owner_total * slot_cap
    sel = (slot[:, :, None] == jnp.arange(slots, dtype=jnp.int32)[None, None, :]).astype(BF16)
    sel = sel.reshape(blocks, block_rows, own_count, slots)
    place = jnp.sum(sel, axis=2)
    return sel, place


def split_hi_lo(x):
    hi = lax.reduce_precision(x, exponent_bits=8, mantissa_bits=7)
    return hi.astype(BF16), (x - hi).astype(BF16)


def local(acts, owner_ids, block_codes, weights, enc_bias, dec_bias):
    dp_count = lax.axis_size(DP)
    dh_count = lax.axis_size("dh")
    dm_count = lax.axis_size("dm")
    dn_count = lax.axis_size("dn")
    lat_count = lax.axis_size("lat")
    dp_idx = (lax.axis_index("dh") * dm_count + lax.axis_index("dm")) * dn_count + lax.axis_index(
        "dn"
    )
    lat_idx = lax.axis_index("lat")
    me = dp_idx * lat_count + lat_idx
    owner_total = dp_count * lat_count
    tok_rows, own_count = owner_ids.shape
    half = acts.shape[1]
    full_width = weights.shape[1]
    lat_own = weights.shape[0]
    block_width = lat_own // BLK_DEV
    fs = half // dp_count
    mine_rows = tok_rows // lat_count
    tokens = tok_rows * dp_count
    blocks = dp_count
    slot_cap = max(2, 2 * tok_rows * own_count // owner_total)

    def rs_tokens(x):
        tail = x.shape[1:]
        y = x.reshape((dp_count, lat_count, mine_rows) + tail).swapaxes(0, 1)
        y = jnp.sum(lax.all_to_all(y, "lat", 0, 0, tiled=True), axis=0)
        y = y.reshape((dh_count, dm_count, dn_count) + y.shape[1:])
        y = jnp.moveaxis(y, 2, 0)
        y = jnp.sum(lax.all_to_all(y, "dn", 0, 0, tiled=True), axis=0).swapaxes(0, 1)
        y = jnp.sum(lax.all_to_all(y, "dm", 0, 0, tiled=True), axis=0)
        return jnp.sum(lax.all_to_all(y, "dh", 0, 0, tiled=True), axis=0)

    def ag_tokens(x):
        y = lax.all_to_all(jnp.broadcast_to(x[None], (dh_count,) + x.shape), "dh", 0, 0, tiled=True)
        y = lax.all_to_all(
            jnp.broadcast_to(y[None], (dm_count,) + y.shape), "dm", 0, 0, tiled=True
        )
        y = lax.all_to_all(
            jnp.broadcast_to(y[None], (dn_count,) + y.shape), "dn", 0, 0, tiled=True
        )
        y = jnp.moveaxis(y, 0, 2).swapaxes(0, 1).reshape((dp_count,) + x.shape)
        y = lax.all_gather(y, "lat", axis=1, tiled=False)
        return y.reshape((tokens,) + x.shape[1:])

    id_vals = tok_rows * own_count * 2
    id_rows = -(-id_vals // fs)
    id_code = jnp.concatenate([owner_ids // 16, owner_ids % 16], axis=1).astype(BF16).reshape(-1)
    id_code = jnp.pad(id_code, (0, id_rows * fs - id_vals)).reshape(id_rows, fs)
    acts_send = jnp.concatenate(
        [
            acts.reshape(tok_rows, dp_count, fs).transpose(1, 0, 2),
            jnp.broadcast_to(id_code[None], (dp_count, id_rows, fs)),
        ],
        axis=1,
    )
    acts_got = lax.all_to_all(acts_send, DP, 0, 0, tiled=True)
    acts_fs = acts_got[:, :tok_rows]
    id_got = acts_got[:, tok_rows:].reshape(dp_count, id_rows * fs)[:, :id_vals]
    id_got = id_got.astype(jnp.int32).reshape(dp_count, tok_rows, 2, own_count)
    ids_all = (id_got[:, :, 0] * 16 + id_got[:, :, 1]).reshape(tokens, own_count)
    w_send = (
        weights.reshape(lat_own, lat_count, dp_count, fs)
        .transpose(2, 1, 0, 3)
        .reshape(owner_total, lat_own, fs)
    )
    w_fs = lax.all_to_all(w_send, ALL, 0, 0, tiled=True)

    sel, place = slot_tables(ids_all, owner_total, tok_rows, slot_cap)

    def rows_to_slots(x_fs):
        y = jnp.einsum("btq,btf->bqf", place, x_fs, preferred_element_type=F32).astype(BF16)
        return y.reshape(blocks, owner_total, slot_cap, fs)

    def slots_to_pairs(v):
        v = v.reshape(blocks, owner_total * slot_cap, -1)
        width = v.shape[-1]
        both = jnp.concatenate(split_hi_lo(v), axis=-1)
        out = jnp.einsum("btkq,bql->btkl", sel, both, preferred_element_type=F32)
        out = out[..., :width] + out[..., width:]
        return out.reshape(tokens, own_count, width)

    def pairs_to_slots(x):
        x = x.reshape(blocks, tok_rows, own_count, -1)
        y = jnp.einsum("btkq,btkl->bql", sel, x, preferred_element_type=F32).astype(BF16)
        return y.reshape(blocks, owner_total, slot_cap, -1)

    acts_slots = rows_to_slots(acts_fs)
    pre_part = jnp.einsum("borf,olf->borl", acts_slots, w_fs, preferred_element_type=F32)
    own_bias = jnp.where(
        (jnp.arange(owner_total) == me)[:, None], enc_bias[None, :], 0.0
    )
    pre_part = pre_part + own_bias[None, :, None, :]
    pre = rs_tokens(slots_to_pairs(pre_part))

    start = lat_idx * mine_rows
    my_ids = lax.dynamic_slice_in_dim(owner_ids, start, mine_rows, 0)
    my_codes = lax.dynamic_slice_in_dim(block_codes, start, mine_rows, 0)
    lat_block = jnp.arange(lat_own, dtype=jnp.int32) // block_width
    gate = ((my_codes[:, :, None] // (2**lat_block)[None, None, :]) % 2).astype(F32)
    codes = (jnp.maximum(pre, 0.0) * gate).astype(BF16)

    codes_slots = pairs_to_slots(ag_tokens(codes))
    contrib = jnp.einsum("borl,olf->borf", codes_slots, w_fs, preferred_element_type=F32)
    contrib = contrib.astype(BF16).reshape(blocks, owner_total * slot_cap, fs)
    summed = jnp.einsum("btq,bqf->btf", place, contrib, preferred_element_type=F32)
    bias_fs = lax.dynamic_slice_in_dim(dec_bias, dp_idx * fs, fs, 0)
    full = summed + bias_fs[None, None, :]
    err = full - acts_fs.astype(F32)
    gerr = err.astype(BF16)
    gdb = jnp.stack(split_hi_lo(jnp.sum(err, axis=(0, 1))))
    recon_send = jnp.concatenate(
        [full.astype(BF16), jnp.broadcast_to(gdb[None], (dp_count, 2, fs))], axis=1
    )
    recon_got = lax.all_to_all(recon_send, DP, 0, 0, tiled=True)
    recon = recon_got[:, :tok_rows].transpose(1, 0, 2).reshape(tok_rows, half)
    gdb_got = recon_got[:, tok_rows:].astype(F32)
    grad_dec_bias = (gdb_got[:, 0] + gdb_got[:, 1]).reshape(half)

    gerr_slots = rows_to_slots(gerr)
    gc_part = jnp.einsum("borf,olf->borl", gerr_slots, w_fs, preferred_element_type=F32)
    gcodes = rs_tokens(slots_to_pairs(gc_part))
    gpre = gcodes * gate * (pre > 0.0).astype(F32)
    own_hit = (
        my_ids[:, :, None] == jnp.arange(owner_total, dtype=jnp.int32)[None, None, :]
    ).astype(F32)
    genc_part = jnp.sum(own_hit[:, :, :, None] * gpre[:, :, None, :], axis=(0, 1))

    gpre_slots = pairs_to_slots(ag_tokens(gpre.astype(BF16)))
    gw = jnp.einsum("borl,borf->olf", codes_slots, gerr_slots, preferred_element_type=F32)
    gw = gw + jnp.einsum("borl,borf->olf", gpre_slots, acts_slots, preferred_element_type=F32)
    enc_vals = 2 * lat_own
    enc_rows = -(-enc_vals // fs)
    genc = jnp.concatenate(split_hi_lo(genc_part), axis=1)
    genc = jnp.pad(genc, ((0, 0), (0, enc_rows * fs - enc_vals))).reshape(owner_total, enc_rows, fs)
    gw_got = lax.all_to_all(
        jnp.concatenate([gw.astype(BF16), genc], axis=1), ALL, 0, 0, tiled=True
    )
    gw_back = gw_got[:, :lat_own]
    genc_got = gw_got[:, lat_own:].reshape(owner_total, enc_rows * fs)[:, :enc_vals].astype(F32)
    grad_enc_bias = jnp.sum(genc_got[:, :lat_own] + genc_got[:, lat_own:], axis=0)
    grad_weights = (
        gw_back.reshape(dp_count, lat_count, lat_own, fs)
        .transpose(2, 1, 0, 3)
        .reshape(lat_own, full_width)
    )
    return (recon, grad_weights, grad_enc_bias, grad_dec_bias)


def solution(mesh):
    dp_count, lat_count = mesh.devices.shape
    halves = 2 if dp_count % 4 == 0 else 1
    split = Mesh(
        mesh.devices.reshape(halves, halves, dp_count // halves // halves, lat_count),
        ("dh", "dm", "dn", "lat"),
    )
    in_specs = (
        P(DP, "lat"),
        P(DP, None),
        P(DP, None),
        P(ALL, None),
        P(ALL),
        P("lat"),
    )
    out_specs = (P(DP, "lat"), P(ALL, None), P(ALL), P("lat"))
    return jax.shard_map(local, mesh=split, in_specs=in_specs, out_specs=out_specs, check_vma=False)
```

```python
import jax
import jax.numpy as jnp
from jax import lax
from jax.sharding import Mesh, PartitionSpec as P

BLK_DEV = 2
DP = ("dh", "dl")
ALL = ("dh", "dl", "lat")
F32 = jnp.float32
BF16 = jnp.bfloat16


def slot_tables(ids, owner_total, block_rows, slot_cap):
    tokens, own_count = ids.shape
    blocks = tokens // block_rows
    onehot = (ids[:, :, None] == jnp.arange(owner_total, dtype=jnp.int32)[None, None, :]).astype(
        jnp.int32
    )
    present = jnp.sum(onehot, axis=1).reshape(blocks, block_rows, owner_total)
    before = (jnp.cumsum(present, axis=1) - present).reshape(tokens, owner_total)
    rank = jnp.sum(onehot * before[:, None, :], axis=2)
    slot = ids * slot_cap + rank
    slots = owner_total * slot_cap
    sel = (slot[:, :, None] == jnp.arange(slots, dtype=jnp.int32)[None, None, :]).astype(BF16)
    sel = sel.reshape(blocks, block_rows, own_count, slots)
    place = jnp.sum(sel, axis=2)
    return sel, place


def split_hi_lo(x):
    hi = lax.reduce_precision(x, exponent_bits=8, mantissa_bits=7)
    return hi.astype(BF16), (x - hi).astype(BF16)


def local(acts, owner_ids, block_codes, weights, enc_bias, dec_bias):
    dp_count = lax.axis_size(DP)
    dh_count = lax.axis_size("dh")
    dl_count = lax.axis_size("dl")
    lat_count = lax.axis_size("lat")
    dp_idx = lax.axis_index("dh") * dl_count + lax.axis_index("dl")
    lat_idx = lax.axis_index("lat")
    me = dp_idx * lat_count + lat_idx
    owner_total = dp_count * lat_count
    tok_rows, own_count = owner_ids.shape
    half = acts.shape[1]
    full_width = weights.shape[1]
    lat_own = weights.shape[0]
    block_width = lat_own // BLK_DEV
    fs = half // dp_count
    mine_rows = tok_rows // lat_count
    tokens = tok_rows * dp_count
    blocks = dp_count
    slot_cap = max(2, 2 * tok_rows * own_count // owner_total)

    def rs_tokens(x):
        tail = x.shape[1:]
        y = x.reshape((dp_count, lat_count, mine_rows) + tail).swapaxes(0, 1)
        y = jnp.sum(lax.all_to_all(y, "lat", 0, 0, tiled=True), axis=0)
        y = y.reshape((dh_count, dl_count) + y.shape[1:]).swapaxes(0, 1)
        y = jnp.sum(lax.all_to_all(y, "dl", 0, 0, tiled=True), axis=0)
        return jnp.sum(lax.all_to_all(y, "dh", 0, 0, tiled=True), axis=0)

    def ag_tokens(x):
        y = lax.all_to_all(jnp.broadcast_to(x[None], (dh_count,) + x.shape), "dh", 0, 0, tiled=True)
        y = lax.all_to_all(
            jnp.broadcast_to(y[None], (dl_count,) + y.shape), "dl", 0, 0, tiled=True
        ).swapaxes(0, 1)
        y = y.reshape((dp_count,) + x.shape)
        y = lax.all_to_all(
            jnp.broadcast_to(y[None], (lat_count,) + y.shape), "lat", 0, 0, tiled=True
        ).swapaxes(0, 1)
        return y.reshape((tokens,) + x.shape[1:])

    id_vals = tok_rows * own_count * 2
    id_rows = -(-id_vals // fs)
    id_code = jnp.concatenate([owner_ids // 16, owner_ids % 16], axis=1).astype(BF16).reshape(-1)
    id_code = jnp.pad(id_code, (0, id_rows * fs - id_vals)).reshape(id_rows, fs)
    acts_send = jnp.concatenate(
        [
            acts.reshape(tok_rows, dp_count, fs).transpose(1, 0, 2),
            jnp.broadcast_to(id_code[None], (dp_count, id_rows, fs)),
        ],
        axis=1,
    )
    acts_got = lax.all_to_all(acts_send, DP, 0, 0, tiled=True)
    acts_fs = acts_got[:, :tok_rows]
    id_got = acts_got[:, tok_rows:].reshape(dp_count, id_rows * fs)[:, :id_vals]
    id_got = id_got.astype(jnp.int32).reshape(dp_count, tok_rows, 2, own_count)
    ids_all = (id_got[:, :, 0] * 16 + id_got[:, :, 1]).reshape(tokens, own_count)
    w_send = (
        weights.reshape(lat_own, lat_count, dp_count, fs)
        .transpose(2, 1, 0, 3)
        .reshape(owner_total, lat_own, fs)
    )
    w_fs = lax.all_to_all(w_send, ALL, 0, 0, tiled=True)

    sel, place = slot_tables(ids_all, owner_total, tok_rows, slot_cap)

    def rows_to_slots(x_fs):
        y = jnp.einsum("btq,btf->bqf", place, x_fs, preferred_element_type=F32).astype(BF16)
        return y.reshape(blocks, owner_total, slot_cap, fs)

    def slots_to_pairs(v):
        v = v.reshape(blocks, owner_total * slot_cap, -1)
        width = v.shape[-1]
        both = jnp.concatenate(split_hi_lo(v), axis=-1)
        out = jnp.einsum("btkq,bql->btkl", sel, both, preferred_element_type=F32)
        out = out[..., :width] + out[..., width:]
        return out.reshape(tokens, own_count, width)

    def pairs_to_slots(x):
        x = x.reshape(blocks, tok_rows, own_count, -1)
        y = jnp.einsum("btkq,btkl->bql", sel, x, preferred_element_type=F32).astype(BF16)
        return y.reshape(blocks, owner_total, slot_cap, -1)

    acts_slots = rows_to_slots(acts_fs)
    pre_part = jnp.einsum("borf,olf->borl", acts_slots, w_fs, preferred_element_type=F32)
    own_bias = jnp.where(
        (jnp.arange(owner_total) == me)[:, None], enc_bias[None, :], 0.0
    )
    pre_part = pre_part + own_bias[None, :, None, :]
    pre = rs_tokens(slots_to_pairs(pre_part))

    start = lat_idx * mine_rows
    my_ids = lax.dynamic_slice_in_dim(owner_ids, start, mine_rows, 0)
    my_codes = lax.dynamic_slice_in_dim(block_codes, start, mine_rows, 0)
    lat_block = jnp.arange(lat_own, dtype=jnp.int32) // block_width
    gate = ((my_codes[:, :, None] // (2**lat_block)[None, None, :]) % 2).astype(F32)
    codes = (jnp.maximum(pre, 0.0) * gate).astype(BF16)

    codes_slots = pairs_to_slots(ag_tokens(codes))
    contrib = jnp.einsum("borl,olf->borf", codes_slots, w_fs, preferred_element_type=F32)
    contrib = contrib.astype(BF16).reshape(blocks, owner_total * slot_cap, fs)
    summed = jnp.einsum("btq,bqf->btf", place, contrib, preferred_element_type=F32)
    bias_fs = lax.dynamic_slice_in_dim(dec_bias, dp_idx * fs, fs, 0)
    full = summed + bias_fs[None, None, :]
    err = full - acts_fs.astype(F32)
    gerr = err.astype(BF16)
    gdb = jnp.stack(split_hi_lo(jnp.sum(err, axis=(0, 1))))
    recon_send = jnp.concatenate(
        [full.astype(BF16), jnp.broadcast_to(gdb[None], (dp_count, 2, fs))], axis=1
    )
    recon_got = lax.all_to_all(recon_send, DP, 0, 0, tiled=True)
    recon = recon_got[:, :tok_rows].transpose(1, 0, 2).reshape(tok_rows, half)
    gdb_got = recon_got[:, tok_rows:].astype(F32)
    grad_dec_bias = (gdb_got[:, 0] + gdb_got[:, 1]).reshape(half)

    gerr_slots = rows_to_slots(gerr)
    gc_part = jnp.einsum("borf,olf->borl", gerr_slots, w_fs, preferred_element_type=F32)
    gcodes = rs_tokens(slots_to_pairs(gc_part))
    gpre = gcodes * gate * (pre > 0.0).astype(F32)
    own_hit = (
        my_ids[:, :, None] == jnp.arange(owner_total, dtype=jnp.int32)[None, None, :]
    ).astype(F32)
    genc_part = jnp.sum(own_hit[:, :, :, None] * gpre[:, :, None, :], axis=(0, 1))

    gpre_slots = pairs_to_slots(ag_tokens(gpre.astype(BF16)))
    gw = jnp.einsum("borl,borf->olf", codes_slots, gerr_slots, preferred_element_type=F32)
    gw = gw + jnp.einsum("borl,borf->olf", gpre_slots, acts_slots, preferred_element_type=F32)
    enc_vals = 2 * lat_own
    enc_rows = -(-enc_vals // fs)
    genc = jnp.concatenate(split_hi_lo(genc_part), axis=1)
    genc = jnp.pad(genc, ((0, 0), (0, enc_rows * fs - enc_vals))).reshape(owner_total, enc_rows, fs)
    gw_got = lax.all_to_all(
        jnp.concatenate([gw.astype(BF16), genc], axis=1), ALL, 0, 0, tiled=True
    )
    gw_back = gw_got[:, :lat_own]
    genc_got = gw_got[:, lat_own:].reshape(owner_total, enc_rows * fs)[:, :enc_vals].astype(F32)
    grad_enc_bias = jnp.sum(genc_got[:, :lat_own] + genc_got[:, lat_own:], axis=0)
    grad_weights = (
        gw_back.reshape(dp_count, lat_count, lat_own, fs)
        .transpose(2, 1, 0, 3)
        .reshape(lat_own, full_width)
    )
    return (recon, grad_weights, grad_enc_bias, grad_dec_bias)


def solution(mesh):
    dp_count, lat_count = mesh.devices.shape
    halves = 2 if dp_count % 2 == 0 else 1
    split = Mesh(mesh.devices.reshape(halves, dp_count // halves, lat_count), ("dh", "dl", "lat"))
    in_specs = (
        P(DP, "lat"),
        P(DP, None),
        P(DP, None),
        P(ALL, None),
        P(ALL),
        P("lat"),
    )
    out_specs = (P(DP, "lat"), P(ALL, None), P(ALL), P("lat"))
    return jax.shard_map(local, mesh=split, in_specs=in_specs, out_specs=out_specs, check_vma=False)
```

```python
import jax
import jax.numpy as jnp
from jax import lax
from jax.sharding import Mesh, PartitionSpec as P

BLK_DEV = 2
DP = ("dh", "dl")
ALL = ("dh", "dl", "lat")
F32 = jnp.float32
BF16 = jnp.bfloat16


def slot_tables(ids, owner_total, block_rows, slot_cap):
    tokens, own_count = ids.shape
    blocks = tokens // block_rows
    onehot = (ids[:, :, None] == jnp.arange(owner_total, dtype=jnp.int32)[None, None, :]).astype(
        jnp.int32
    )
    present = jnp.sum(onehot, axis=1).reshape(blocks, block_rows, owner_total)
    before = (jnp.cumsum(present, axis=1) - present).reshape(tokens, owner_total)
    rank = jnp.sum(onehot * before[:, None, :], axis=2)
    slot = ids * slot_cap + rank
    slots = owner_total * slot_cap
    sel = (slot[:, :, None] == jnp.arange(slots, dtype=jnp.int32)[None, None, :]).astype(BF16)
    sel = sel.reshape(blocks, block_rows, own_count, slots)
    place = jnp.sum(sel, axis=2)
    return sel, place


def split_hi_lo(x):
    hi = lax.reduce_precision(x, exponent_bits=8, mantissa_bits=7)
    return hi.astype(BF16), (x - hi).astype(BF16)


def local(acts, owner_ids, block_codes, weights, enc_bias, dec_bias):
    dp_count = lax.axis_size(DP)
    dh_count = lax.axis_size("dh")
    dl_count = lax.axis_size("dl")
    lat_count = lax.axis_size("lat")
    dp_idx = lax.axis_index("dh") * dl_count + lax.axis_index("dl")
    lat_idx = lax.axis_index("lat")
    me = dp_idx * lat_count + lat_idx
    owner_total = dp_count * lat_count
    tok_rows, own_count = owner_ids.shape
    half = acts.shape[1]
    full_width = weights.shape[1]
    lat_own = weights.shape[0]
    block_width = lat_own // BLK_DEV
    fs = half // dp_count
    mine_rows = tok_rows // lat_count
    tokens = tok_rows * dp_count
    blocks = dp_count
    slot_cap = max(2, 2 * tok_rows * own_count // owner_total)

    def rs_tokens(x):
        tail = x.shape[1:]
        y = x.reshape((dp_count, lat_count, mine_rows) + tail).swapaxes(0, 1)
        y = jnp.sum(lax.all_to_all(y, "lat", 0, 0, tiled=True), axis=0)
        y = y.reshape((dh_count, dl_count) + y.shape[1:]).swapaxes(0, 1)
        y = jnp.sum(lax.all_to_all(y, "dl", 0, 0, tiled=True), axis=0)
        return jnp.sum(lax.all_to_all(y, "dh", 0, 0, tiled=True), axis=0)

    def ag_tokens(x):
        y = lax.all_to_all(jnp.broadcast_to(x[None], (dh_count,) + x.shape), "dh", 0, 0, tiled=True)
        y = lax.all_to_all(
            jnp.broadcast_to(y[None], (dl_count,) + y.shape), "dl", 0, 0, tiled=True
        ).swapaxes(0, 1)
        y = y.reshape((dp_count,) + x.shape)
        y = lax.all_to_all(
            jnp.broadcast_to(y[None], (lat_count,) + y.shape), "lat", 0, 0, tiled=True
        ).swapaxes(0, 1)
        return y.reshape((tokens,) + x.shape[1:])

    id_vals = tok_rows * own_count * 2
    id_rows = -(-id_vals // fs)
    id_code = jnp.concatenate([owner_ids // 16, owner_ids % 16], axis=1).astype(BF16).reshape(-1)
    id_code = jnp.pad(id_code, (0, id_rows * fs - id_vals)).reshape(id_rows, fs)
    acts_send = jnp.concatenate(
        [
            acts.reshape(tok_rows, dp_count, fs).transpose(1, 0, 2),
            jnp.broadcast_to(id_code[None], (dp_count, id_rows, fs)),
        ],
        axis=1,
    )
    acts_got = lax.all_to_all(acts_send, DP, 0, 0, tiled=True)
    acts_fs = acts_got[:, :tok_rows]
    id_got = acts_got[:, tok_rows:].reshape(dp_count, id_rows * fs)[:, :id_vals]
    id_got = id_got.astype(jnp.int32).reshape(dp_count, tok_rows, 2, own_count)
    ids_all = (id_got[:, :, 0] * 16 + id_got[:, :, 1]).reshape(tokens, own_count)
    w_send = (
        weights.reshape(lat_own, lat_count, dp_count, fs)
        .transpose(2, 1, 0, 3)
        .reshape(owner_total, lat_own, fs)
    )
    bias_vals = 2 * lat_own
    bias_rows = -(-bias_vals // fs)
    bias_code = jnp.concatenate(split_hi_lo(enc_bias), axis=0)
    bias_code = jnp.pad(bias_code, (0, bias_rows * fs - bias_vals)).reshape(bias_rows, fs)
    w_send = jnp.concatenate(
        [w_send, jnp.broadcast_to(bias_code[None], (owner_total, bias_rows, fs))], axis=1
    )
    w_got = lax.all_to_all(w_send, ALL, 0, 0, tiled=True)
    w_fs = w_got[:, :lat_own]
    bias_got = w_got[:, lat_own:].reshape(owner_total, bias_rows * fs)[:, :bias_vals].astype(F32)
    enc_all = bias_got[:, :lat_own] + bias_got[:, lat_own:]

    sel, place = slot_tables(ids_all, owner_total, tok_rows, slot_cap)

    def rows_to_slots(x_fs):
        y = jnp.einsum("btq,btf->bqf", place, x_fs, preferred_element_type=F32).astype(BF16)
        return y.reshape(blocks, owner_total, slot_cap, fs)

    def slots_to_pairs(v):
        v = v.reshape(blocks, owner_total * slot_cap, -1)
        width = v.shape[-1]
        both = jnp.concatenate(split_hi_lo(v), axis=-1)
        out = jnp.einsum("btkq,bql->btkl", sel, both, preferred_element_type=F32)
        out = out[..., :width] + out[..., width:]
        return out.reshape(tokens, own_count, width)

    def pairs_to_slots(x):
        x = x.reshape(blocks, tok_rows, own_count, -1)
        y = jnp.einsum("btkq,btkl->bql", sel, x, preferred_element_type=F32).astype(BF16)
        return y.reshape(blocks, owner_total, slot_cap, -1)

    acts_slots = rows_to_slots(acts_fs)
    pre_part = jnp.einsum("borf,olf->borl", acts_slots, w_fs, preferred_element_type=F32)

    start = lat_idx * mine_rows
    my_ids = lax.dynamic_slice_in_dim(owner_ids, start, mine_rows, 0)
    my_codes = lax.dynamic_slice_in_dim(block_codes, start, mine_rows, 0)
    own_hit = (
        my_ids[:, :, None] == jnp.arange(owner_total, dtype=jnp.int32)[None, None, :]
    ).astype(F32)
    pair_bias = jnp.sum(own_hit[:, :, :, None] * enc_all[None, None, :, :], axis=2)
    pre = rs_tokens(slots_to_pairs(pre_part)) + pair_bias
    lat_block = jnp.arange(lat_own, dtype=jnp.int32) // block_width
    gate = ((my_codes[:, :, None] // (2**lat_block)[None, None, :]) % 2).astype(F32)
    codes = (jnp.maximum(pre, 0.0) * gate).astype(BF16)

    codes_slots = pairs_to_slots(ag_tokens(codes))
    contrib = jnp.einsum("borl,olf->borf", codes_slots, w_fs, preferred_element_type=F32)
    contrib = contrib.astype(BF16).reshape(blocks, owner_total * slot_cap, fs)
    summed = jnp.einsum("btq,bqf->btf", place, contrib, preferred_element_type=F32)
    bias_fs = lax.dynamic_slice_in_dim(dec_bias, dp_idx * fs, fs, 0)
    full = summed + bias_fs[None, None, :]
    err = full - acts_fs.astype(F32)
    gerr = err.astype(BF16)
    gdb = jnp.stack(split_hi_lo(jnp.sum(err, axis=(0, 1))))
    recon_send = jnp.concatenate(
        [full.astype(BF16), jnp.broadcast_to(gdb[None], (dp_count, 2, fs))], axis=1
    )
    recon_got = lax.all_to_all(recon_send, DP, 0, 0, tiled=True)
    recon = recon_got[:, :tok_rows].transpose(1, 0, 2).reshape(tok_rows, half)
    gdb_got = recon_got[:, tok_rows:].astype(F32)
    grad_dec_bias = (gdb_got[:, 0] + gdb_got[:, 1]).reshape(half)

    gerr_slots = rows_to_slots(gerr)
    gc_part = jnp.einsum("borf,olf->borl", gerr_slots, w_fs, preferred_element_type=F32)
    gcodes = rs_tokens(slots_to_pairs(gc_part))
    gpre = gcodes * gate * (pre > 0.0).astype(F32)
    genc_part = jnp.sum(own_hit[:, :, :, None] * gpre[:, :, None, :], axis=(0, 1))

    gpre_slots = pairs_to_slots(ag_tokens(gpre.astype(BF16)))
    gw = jnp.einsum("borl,borf->olf", codes_slots, gerr_slots, preferred_element_type=F32)
    gw = gw + jnp.einsum("borl,borf->olf", gpre_slots, acts_slots, preferred_element_type=F32)
    enc_vals = 2 * lat_own
    enc_rows = -(-enc_vals // fs)
    genc = jnp.concatenate(split_hi_lo(genc_part), axis=1)
    genc = jnp.pad(genc, ((0, 0), (0, enc_rows * fs - enc_vals))).reshape(owner_total, enc_rows, fs)
    gw_got = lax.all_to_all(
        jnp.concatenate([gw.astype(BF16), genc], axis=1), ALL, 0, 0, tiled=True
    )
    gw_back = gw_got[:, :lat_own]
    genc_got = gw_got[:, lat_own:].reshape(owner_total, enc_rows * fs)[:, :enc_vals].astype(F32)
    grad_enc_bias = jnp.sum(genc_got[:, :lat_own] + genc_got[:, lat_own:], axis=0)
    grad_weights = (
        gw_back.reshape(dp_count, lat_count, lat_own, fs)
        .transpose(2, 1, 0, 3)
        .reshape(lat_own, full_width)
    )
    return (recon, grad_weights, grad_enc_bias, grad_dec_bias)


def solution(mesh):
    dp_count, lat_count = mesh.devices.shape
    halves = 2 if dp_count % 2 == 0 else 1
    split = Mesh(mesh.devices.reshape(halves, dp_count // halves, lat_count), ("dh", "dl", "lat"))
    in_specs = (
        P(DP, "lat"),
        P(DP, None),
        P(DP, None),
        P(ALL, None),
        P(ALL),
        P("lat"),
    )
    out_specs = (P(DP, "lat"), P(ALL, None), P(ALL), P("lat"))
    return jax.shard_map(local, mesh=split, in_specs=in_specs, out_specs=out_specs, check_vma=False)
```

```python
import jax
import jax.numpy as jnp
from jax import lax
from jax.sharding import Mesh, PartitionSpec as P

BLK_DEV = 2
DP = ("dh", "dl")
ALL = ("dh", "dl", "lat")
F32 = jnp.float32
BF16 = jnp.bfloat16


def slot_tables(ids, owner_total, block_rows, slot_cap):
    tokens, own_count = ids.shape
    blocks = tokens // block_rows
    onehot = (ids[:, :, None] == jnp.arange(owner_total, dtype=jnp.int32)[None, None, :]).astype(
        jnp.int32
    )
    present = jnp.sum(onehot, axis=1).reshape(blocks, block_rows, owner_total)
    before = (jnp.cumsum(present, axis=1) - present).reshape(tokens, owner_total)
    rank = jnp.sum(onehot * before[:, None, :], axis=2)
    slot = ids * slot_cap + rank
    slots = owner_total * slot_cap
    sel = (slot[:, :, None] == jnp.arange(slots, dtype=jnp.int32)[None, None, :]).astype(BF16)
    sel = sel.reshape(blocks, block_rows, own_count, slots)
    place = jnp.sum(sel, axis=2)
    return sel, place


def split_hi_lo(x):
    hi = lax.reduce_precision(x, exponent_bits=8, mantissa_bits=7)
    return hi.astype(BF16), (x - hi).astype(BF16)


def local(acts, owner_ids, block_codes, weights, enc_bias, dec_bias):
    dp_count = lax.axis_size(DP)
    dh_count = lax.axis_size("dh")
    dl_count = lax.axis_size("dl")
    lat_count = lax.axis_size("lat")
    dp_idx = lax.axis_index("dh") * dl_count + lax.axis_index("dl")
    lat_idx = lax.axis_index("lat")
    me = dp_idx * lat_count + lat_idx
    owner_total = dp_count * lat_count
    tok_rows, own_count = owner_ids.shape
    half = acts.shape[1]
    full_width = weights.shape[1]
    lat_own = weights.shape[0]
    block_width = lat_own // BLK_DEV
    fs = half // dp_count
    mine_rows = tok_rows // lat_count
    tokens = tok_rows * dp_count
    blocks = dp_count
    slot_cap = max(2, 2 * tok_rows * own_count // owner_total)

    def rs_tokens(x):
        tail = x.shape[1:]
        y = x.reshape((dp_count, lat_count, mine_rows) + tail).swapaxes(0, 1)
        y = jnp.sum(lax.all_to_all(y, "lat", 0, 0, tiled=True), axis=0)
        y = y.reshape((dh_count, dl_count) + y.shape[1:]).swapaxes(0, 1)
        y = jnp.sum(lax.all_to_all(y, "dl", 0, 0, tiled=True), axis=0)
        return jnp.sum(lax.all_to_all(y, "dh", 0, 0, tiled=True), axis=0)

    def ag_tokens(x):
        y = lax.all_to_all(jnp.broadcast_to(x[None], (dh_count,) + x.shape), "dh", 0, 0, tiled=True)
        y = lax.all_to_all(
            jnp.broadcast_to(y[None], (dl_count,) + y.shape), "dl", 0, 0, tiled=True
        ).swapaxes(0, 1)
        y = y.reshape((dp_count,) + x.shape)
        y = lax.all_to_all(
            jnp.broadcast_to(y[None], (lat_count,) + y.shape), "lat", 0, 0, tiled=True
        ).swapaxes(0, 1)
        return y.reshape((tokens,) + x.shape[1:])

    id_vals = tok_rows * own_count * 2
    id_rows = -(-id_vals // fs)
    id_code = jnp.concatenate([owner_ids // 16, owner_ids % 16], axis=1).astype(BF16).reshape(-1)
    id_code = jnp.pad(id_code, (0, id_rows * fs - id_vals)).reshape(id_rows, fs)
    acts_send = jnp.concatenate(
        [
            acts.reshape(tok_rows, dp_count, fs).transpose(1, 0, 2),
            jnp.broadcast_to(id_code[None], (dp_count, id_rows, fs)),
        ],
        axis=1,
    )
    acts_got = lax.all_to_all(acts_send, DP, 0, 0, tiled=True)
    acts_fs = acts_got[:, :tok_rows]
    id_got = acts_got[:, tok_rows:].reshape(dp_count, id_rows * fs)[:, :id_vals]
    id_got = id_got.astype(jnp.int32).reshape(dp_count, tok_rows, 2, own_count)
    ids_all = (id_got[:, :, 0] * 16 + id_got[:, :, 1]).reshape(tokens, own_count)
    w_send = (
        weights.reshape(lat_own, lat_count, dp_count, fs)
        .transpose(2, 1, 0, 3)
        .reshape(owner_total, lat_own, fs)
    )
    w_fs = lax.all_to_all(w_send, ALL, 0, 0, tiled=True)

    sel, place = slot_tables(ids_all, owner_total, tok_rows, slot_cap)

    def rows_to_slots(x_fs):
        y = jnp.einsum("btq,btf->bqf", place, x_fs, preferred_element_type=F32).astype(BF16)
        return y.reshape(blocks, owner_total, slot_cap, fs)

    def slots_to_pairs(v):
        v = v.reshape(blocks, owner_total * slot_cap, -1)
        width = v.shape[-1]
        both = jnp.concatenate(split_hi_lo(v), axis=-1)
        out = jnp.einsum("btkq,bql->btkl", sel, both, preferred_element_type=F32)
        out = out[..., :width] + out[..., width:]
        return out.reshape(tokens, own_count, width)

    def pairs_to_slots(x):
        x = x.reshape(blocks, tok_rows, own_count, -1)
        y = jnp.einsum("btkq,btkl->bql", sel, x, preferred_element_type=F32).astype(BF16)
        return y.reshape(blocks, owner_total, slot_cap, -1)

    acts_slots = rows_to_slots(acts_fs)
    pre_part = jnp.einsum("borf,olf->borl", acts_slots, w_fs, preferred_element_type=F32)
    own_bias = jnp.where((ids_all == me)[:, :, None], enc_bias[None, None, :], 0.0)
    pre = rs_tokens(slots_to_pairs(pre_part) + own_bias)

    start = lat_idx * mine_rows
    my_ids = lax.dynamic_slice_in_dim(owner_ids, start, mine_rows, 0)
    my_codes = lax.dynamic_slice_in_dim(block_codes, start, mine_rows, 0)
    lat_block = jnp.arange(lat_own, dtype=jnp.int32) // block_width
    gate = ((my_codes[:, :, None] // (2**lat_block)[None, None, :]) % 2).astype(F32)
    codes = (jnp.maximum(pre, 0.0) * gate).astype(BF16)

    codes_slots = pairs_to_slots(ag_tokens(codes))
    contrib = jnp.einsum("borl,olf->borf", codes_slots, w_fs, preferred_element_type=F32)
    contrib = contrib.astype(BF16).reshape(blocks, owner_total * slot_cap, fs)
    summed = jnp.einsum("btq,bqf->btf", place, contrib, preferred_element_type=F32)
    bias_fs = lax.dynamic_slice_in_dim(dec_bias, dp_idx * fs, fs, 0)
    full = summed + bias_fs[None, None, :]
    err = full - acts_fs.astype(F32)
    gerr = err.astype(BF16)
    gdb = jnp.stack(split_hi_lo(jnp.sum(err, axis=(0, 1))))
    recon_send = jnp.concatenate(
        [full.astype(BF16), jnp.broadcast_to(gdb[None], (dp_count, 2, fs))], axis=1
    )
    recon_got = lax.all_to_all(recon_send, DP, 0, 0, tiled=True)
    recon = recon_got[:, :tok_rows].transpose(1, 0, 2).reshape(tok_rows, half)
    gdb_got = recon_got[:, tok_rows:].astype(F32)
    grad_dec_bias = (gdb_got[:, 0] + gdb_got[:, 1]).reshape(half)

    gerr_slots = rows_to_slots(gerr)
    gc_part = jnp.einsum("borf,olf->borl", gerr_slots, w_fs, preferred_element_type=F32)
    gcodes = rs_tokens(slots_to_pairs(gc_part))
    gpre = gcodes * gate * (pre > 0.0).astype(F32)
    own_hit = (
        my_ids[:, :, None] == jnp.arange(owner_total, dtype=jnp.int32)[None, None, :]
    ).astype(F32)
    genc_part = jnp.sum(own_hit[:, :, :, None] * gpre[:, :, None, :], axis=(0, 1))

    gpre_slots = pairs_to_slots(ag_tokens(gpre.astype(BF16)))
    gw = jnp.einsum("borl,borf->olf", codes_slots, gerr_slots, preferred_element_type=F32)
    gw = gw + jnp.einsum("borl,borf->olf", gpre_slots, acts_slots, preferred_element_type=F32)
    enc_vals = 2 * lat_own
    enc_rows = -(-enc_vals // fs)
    genc = jnp.concatenate(split_hi_lo(genc_part), axis=1)
    genc = jnp.pad(genc, ((0, 0), (0, enc_rows * fs - enc_vals))).reshape(owner_total, enc_rows, fs)
    gw_got = lax.all_to_all(
        jnp.concatenate([gw.astype(BF16), genc], axis=1), ALL, 0, 0, tiled=True
    )
    gw_back = gw_got[:, :lat_own]
    genc_got = gw_got[:, lat_own:].reshape(owner_total, enc_rows * fs)[:, :enc_vals].astype(F32)
    grad_enc_bias = jnp.sum(genc_got[:, :lat_own] + genc_got[:, lat_own:], axis=0)
    grad_weights = (
        gw_back.reshape(dp_count, lat_count, lat_own, fs)
        .transpose(2, 1, 0, 3)
        .reshape(lat_own, full_width)
    )
    return (recon, grad_weights, grad_enc_bias, grad_dec_bias)


def solution(mesh):
    dp_count, lat_count = mesh.devices.shape
    halves = 2 if dp_count % 2 == 0 else 1
    split = Mesh(mesh.devices.reshape(halves, dp_count // halves, lat_count), ("dh", "dl", "lat"))
    in_specs = (
        P(DP, "lat"),
        P(DP, None),
        P(DP, None),
        P(ALL, None),
        P(ALL),
        P("lat"),
    )
    out_specs = (P(DP, "lat"), P(ALL, None), P(ALL), P("lat"))
    return jax.shard_map(local, mesh=split, in_specs=in_specs, out_specs=out_specs, check_vma=False)
```
